512 devices in a mesh: line: 32 (over z, core), scan: 16 (over x, y).
Axes of the slice: x: 4, y: 4, z: 16, core: 2. Of those that a mesh axis runs over, the one named last changes fastest.
Arguments:
- query_row: bfloat16 [32, 2048, 512], P('line', 'scan'), may hold values from -6 to 6
- key_row: bfloat16 [32, 2048, 512], P('line', 'scan'), may hold values from -6 to 6
- value_row: bfloat16 [32, 2048, 512], P('line', 'scan'), may hold values from -6 to 6
- decay_row: float32 [32, 2048, 4], P('line', 'scan'), may hold values from -2 to 0
- beta_row: float32 [32, 2048, 4], P('line', 'scan'), may hold values from 0.02 to 0.2
- gain_row: float32 [128], replicated, may hold values from 0.1 to 1.9
- query_col: bfloat16 [32, 16, 128, 512], P(None, 'scan', 'line'), may hold values from -6 to 6
- key_col: bfloat16 [32, 16, 128, 512], P(None, 'scan', 'line'), may hold values from -6 to 6
- decay_col: float32 [32, 16, 128, 4], P(None, 'scan', 'line'), may hold values from -2 to 0
- beta_col: float32 [32, 16, 128, 4], P(None, 'scan', 'line'), may hold values from 0.02 to 0.2
- gain_col: float32 [128], replicated, may hold values from 0.1 to 1.9
Outputs:
- mixed: bfloat16 [32, 2048, 512], P('line', 'scan')
The draws below stay inside these ranges and needn't reach their ends.
All inputs are finite; a program needn't handle non-finite values.
Results may differ from the reference program's by a relative error of at most 0.0049.
Values may be sent and summed in bfloat16 or wider, within the bound.
No kernel may reach another device: no remote copies, remote signals or barrier semaphores. Data moves between devices by JAX's collectives and lax.ppermute only.
A program may use at most 64 MiB of HBM per device.

```python
import math
import jax
import jax.numpy as jnp
from jax import lax

SEG = 128
HEAD_GROUP = 4
DK = 128
F = 512
H = 32
SEGS = 16
W = 2048
CB = 32


def decay_field(key, leading_count, sequence_length):
    random_subkeys = jax.random.split(key, 6)
    slow_share = 0.5
    choose = jax.random.uniform(random_subkeys[0], (HEAD_GROUP,))
    slow_rate = jnp.exp(jax.random.uniform(random_subkeys[1], (HEAD_GROUP,), minval=-1.6, maxval=0.0)) / sequence_length
    fast_scale = 30.0 * jnp.exp(jax.random.uniform(random_subkeys[2], (HEAD_GROUP,), minval=0.0, maxval=2.302585))
    fast_rate = 1.0 / fast_scale
    baseline_rate = jnp.where(choose < slow_share, slow_rate, fast_rate)
    block_extent = min(SEG, sequence_length)
    number_of_blocks = sequence_length // block_extent
    token_multiplier = jnp.exp(jax.random.uniform(random_subkeys[3], (leading_count, number_of_blocks, block_extent, HEAD_GROUP), minval=-0.7, maxval=0.7))
    block_multiplier = jnp.exp(jax.random.uniform(random_subkeys[4], (leading_count, number_of_blocks, 1, HEAD_GROUP), minval=-0.7, maxval=0.7))
    spike_sample = jax.random.uniform(random_subkeys[5], (2, leading_count, number_of_blocks, block_extent, HEAD_GROUP))
    spike_events = jnp.where(spike_sample[0] < 2.0 / sequence_length, jnp.log(0.5 + 0.3 * spike_sample[1]), 0.0)
    token_grid = -baseline_rate * token_multiplier * block_multiplier + spike_events
    return token_grid.reshape(leading_count, sequence_length, HEAD_GROUP).astype(jnp.float32)


def drawn_keys(key, leading_count, sequence_length):
    random_subkeys = jax.random.split(key, 2)
    shared = jax.random.normal(random_subkeys[0], (leading_count, 1, HEAD_GROUP, DK), dtype=jnp.float32)
    shared_weight = 0.8944272
    noise_weight = 0.4472136
    noise = jax.random.normal(random_subkeys[1], (leading_count, sequence_length, HEAD_GROUP, DK), dtype=jnp.float32)
    field = jnp.clip(shared_weight * shared + noise_weight * noise, -6.0, 6.0)
    return field.reshape(leading_count, sequence_length, HEAD_GROUP * DK).astype(jnp.float32)


def draw_key_row(key, part):
    return drawn_keys(jax.random.fold_in(key, 31), H, W).astype(jnp.bfloat16)


def draw_key_col(key, part):
    field = drawn_keys(jax.random.fold_in(key, 37), W, H)
    return field.transpose(1, 0, 2).reshape(H, SEGS, SEG, HEAD_GROUP * DK).astype(jnp.bfloat16)


def draw_decay_row(key, part):
    return decay_field(jax.random.fold_in(key, 11), H, W)


def draw_decay_col(key, part):
    token_grid = decay_field(jax.random.fold_in(key, 23), W, H)
    return token_grid.transpose(1, 0, 2).reshape(H, SEGS, SEG, HEAD_GROUP)


def block_levels(key, shape, cuts, smallest, top_value):
    loudness, own = 1.0, jax.random.fold_in(key, 6)
    for dim, blocks in cuts:
        draws = jnp.exp(jax.random.uniform(jax.random.fold_in(own, dim), (blocks,), jnp.float32, smallest / len(cuts), top_value / len(cuts)))
        loudness = loudness * jnp.repeat(draws, shape[dim] // blocks).reshape([-1 if axis == dim else 1 for axis in range(len(shape))])
    return loudness


def gaussian(stream_key, dims, deviation, reach, cuts=(), held_as=jnp.bfloat16):
    loudness = block_levels(stream_key, dims, cuts, -0.22, 0.18) if cuts else 1.0
    result = jax.random.normal(stream_key, dims, jnp.float32) * deviation * loudness
    return jnp.minimum(jnp.maximum(result, -reach), reach).astype(held_as)


def setup_inputs(seed: int = 0) -> dict:
    seeds = jax.random.split(jax.random.key(seed), 12)
    query_row = gaussian(seeds[0], (H, W, F), 1.0, 6.0, ((0, 32), (1, 16)))
    key_row = draw_key_row(jax.random.fold_in(seeds[11], 71), 0)
    value_row = gaussian(seeds[2], (H, W, F), 1.0, 6.0, ((0, 32), (1, 16)))
    decay_row = draw_decay_row(jax.random.fold_in(seeds[11], 71), 0)
    beta_row = jnp.clip(jnp.exp(math.log(0.2) - 2.3025851 * jax.random.uniform(seeds[4], (H, W, HEAD_GROUP), jnp.float32) ** block_levels(seeds[4], (H, W, HEAD_GROUP), ((0, 32), (1, 16)), -0.2, 0.2)), 0.02, 0.2)
    gain_row = jnp.clip(1.0 + 0.18 * jax.random.normal(seeds[5], (DK,), jnp.float32), 0.1, 1.9)
    query_col = gaussian(seeds[6], (H, SEGS, SEG, F), 1.0, 6.0, ((1, 16), (2, 32)))
    key_col = draw_key_col(jax.random.fold_in(seeds[11], 71), 0)
    decay_col = draw_decay_col(jax.random.fold_in(seeds[11], 71), 0)
    beta_col = jnp.clip(jnp.exp(math.log(0.2) - 2.3025851 * jax.random.uniform(seeds[9], (H, SEGS, SEG, HEAD_GROUP), jnp.float32) ** block_levels(seeds[9], (H, SEGS, SEG, HEAD_GROUP), ((1, 16), (2, 32)), -0.2, 0.2)), 0.02, 0.2)
    gain_col = jnp.clip(1.0 + 0.18 * jax.random.normal(seeds[10], (DK,), jnp.float32), 0.1, 1.9)
    return {"query_row": query_row, "key_row": key_row, "value_row": value_row, "decay_row": decay_row, "beta_row": beta_row, "gain_row": gain_row, "query_col": query_col, "key_col": key_col, "decay_col": decay_col, "beta_col": beta_col, "gain_col": gain_col}


HIGHEST = lax.Precision.HIGHEST

def block_terms(query_block, key_block, value_block, log_decay, beta_block):
    key_unit = key_block / jnp.sqrt(lax.optimization_barrier(jnp.sum(key_block * key_block, axis=-1, keepdims=True)) + 1e-06)
    cumulative = jnp.cumsum(log_decay, axis=-1)
    sequence_length = key_block.shape[1]
    lower_mask = jnp.tril(jnp.ones((sequence_length, sequence_length), dtype=jnp.bool_))
    strict = jnp.tril(jnp.ones((sequence_length, sequence_length), dtype=jnp.bool_), -1)
    spread = cumulative[:, :, None] - cumulative[:, None, :]
    ratios = jnp.where(lower_mask, jnp.exp(jnp.where(lower_mask, spread, 0.0)), 0.0)
    key_inner = jnp.einsum('bik,bjk->bij', key_unit, key_unit, precision=HIGHEST)
    system = jnp.where(strict, beta_block[:, :, None] * ratios * key_inner, 0.0) + jnp.eye(sequence_length, dtype=jnp.float32)
    growth = jnp.exp(cumulative)
    right_side = jnp.concatenate([beta_block[:, :, None] * value_block, (beta_block * growth)[:, :, None] * key_unit], axis=-1)
    solved = jax.scipy.linalg.solve_triangular(system, right_side, lower=True)
    value_size = value_block.shape[-1]
    updates = solved[:, :, :value_size]
    weighted = solved[:, :, value_size:]
    attend = ratios * jnp.einsum('bik,bjk->bij', query_block, key_unit, precision=HIGHEST)
    local_out = jnp.einsum('bij,bjv->biv', attend, updates, precision=HIGHEST)
    state_query = growth[:, :, None] * query_block - jnp.einsum('bij,bjk->bik', attend, weighted, precision=HIGHEST)
    key_tail = jnp.exp(cumulative[:, -1:] - cumulative)[:, :, None] * key_unit
    return (local_out, state_query, key_tail, weighted, updates, growth[:, -1])

def scan_blocks(queries, key_rows, values, log_decay, beta_rows, block_extent):
    batch_size, sequence_length, head_size = queries.shape
    number_of_blocks = sequence_length // block_extent

    def blocks(array):
        return array.reshape((batch_size, number_of_blocks, block_extent) + array.shape[2:]).swapaxes(0, 1)

    def advance(carried, pieces):
        local_out, state_query, key_tail, weighted, updates, ending = block_terms(*pieces)
        output = local_out + jnp.einsum('bik,bkv->biv', state_query, carried, precision=HIGHEST)
        residue = updates - jnp.einsum('bjk,bkv->bjv', weighted, carried, precision=HIGHEST)
        carried = ending[:, None, None] * carried + jnp.einsum('bjk,bjv->bkv', key_tail, residue, precision=HIGHEST)
        return (carried, output)
    initial = jnp.zeros((batch_size, head_size, head_size), dtype=jnp.float32)
    last_state, outputs = lax.scan(advance, initial, (blocks(queries), blocks(key_rows), blocks(values), blocks(log_decay), blocks(beta_rows)))
    return outputs.swapaxes(0, 1).reshape(batch_size, sequence_length, head_size)

def to_heads(array, leading_count, sequence_length, head_count, head_size):
    shaped = array.astype(jnp.float32).reshape(leading_count, sequence_length, head_count, head_size)
    return shaped.transpose(0, 2, 1, 3).reshape(leading_count * head_count, sequence_length, head_size)

def gates_to_heads(array, leading_count, sequence_length, head_count):
    return array.reshape(leading_count, sequence_length, head_count).transpose(0, 2, 1).reshape(leading_count * head_count, sequence_length)

def from_heads(array, leading_count, sequence_length, head_count, head_size):
    return array.reshape(leading_count, head_count, sequence_length, head_size).transpose(0, 2, 1, 3)

def head_norm(array, gain):
    return array * lax.rsqrt(lax.optimization_barrier(jnp.mean(array * array, axis=-1, keepdims=True)) + 1e-05) * gain

def columns(array):
    return array.reshape(H, W, -1).transpose(1, 0, 2)

def reference(query_row, key_row, value_row, decay_row, beta_row, gain_row, query_col, key_col, decay_col, beta_col, gain_col):
    row_out = scan_blocks(to_heads(query_row, H, W, HEAD_GROUP, DK), to_heads(key_row, H, W, HEAD_GROUP, DK), to_heads(value_row, H, W, HEAD_GROUP, DK), gates_to_heads(decay_row, H, W, HEAD_GROUP), gates_to_heads(beta_row, H, W, HEAD_GROUP), SEG)
    row_scan = from_heads(row_out, H, W, HEAD_GROUP, DK)
    values_col = head_norm(row_scan, gain_row).reshape(H, W, F).astype(jnp.bfloat16)
    values_col = lax.optimization_barrier(values_col)
    col_out = scan_blocks(to_heads(columns(query_col), W, H, HEAD_GROUP, DK), to_heads(columns(key_col), W, H, HEAD_GROUP, DK), to_heads(values_col.transpose(1, 0, 2), W, H, HEAD_GROUP, DK), gates_to_heads(columns(decay_col), W, H, HEAD_GROUP), gates_to_heads(columns(beta_col), W, H, HEAD_GROUP), CB)
    col_scan = from_heads(col_out, W, H, HEAD_GROUP, DK)
    mixed = head_norm(col_scan, gain_col).reshape(W, H, F).transpose(1, 0, 2)
    return mixed.astype(jnp.bfloat16)
```

```python
import jax
import jax.numpy as jnp
from jax import lax
from jax.sharding import PartitionSpec as P

HIGHEST = lax.Precision.HIGHEST
BASE_BLOCK = 16


def from_behind(block, axis, distance):
    devices = range(lax.axis_size(axis))
    route = [(i - distance, i) for i in devices if i - distance in devices]
    return lax.ppermute(block, axis, route)


def matmul(spec, left, right):
    return jnp.einsum(spec, left, right, precision=HIGHEST)


def unit_lower_inverse(system):
    batch = system.shape[:-2]
    size = system.shape[-1]
    base = min(BASE_BLOCK, size)
    count = size // base
    assert count * base == size and count & (count - 1) == 0
    eye = jnp.eye(base, dtype=jnp.float32)
    grid = system.reshape(batch + (count, base, count, base))
    diagonal = jnp.moveaxis(jnp.diagonal(grid, axis1=-4, axis2=-2), -1, -3)
    lower = diagonal - eye
    inverse = eye - lower
    power = lower
    reach = 2
    while reach < base:
        power = matmul("...ij,...jk->...ik", power, power)
        inverse = inverse + matmul("...ij,...jk->...ik", inverse, power)
        reach *= 2
    width = base
    while width < size:
        pairs = size // (2 * width)
        grid = system.reshape(batch + (pairs, 2, width, pairs, 2, width))
        coupling = jnp.moveaxis(jnp.diagonal(grid, axis1=-6, axis2=-3), -1, -5)[..., 1, :, 0, :]
        halves = inverse.reshape(batch + (pairs, 2, width, width))
        upper_inverse = halves[..., 0, :, :]
        lower_inverse = halves[..., 1, :, :]
        mixed = -matmul(
            "...ij,...jk->...ik", matmul("...ij,...jk->...ik", lower_inverse, coupling), upper_inverse
        )
        top = jnp.concatenate([upper_inverse, jnp.zeros_like(upper_inverse)], axis=-1)
        bottom = jnp.concatenate([mixed, lower_inverse], axis=-1)
        inverse = jnp.concatenate([top, bottom], axis=-2)
        width *= 2
    return inverse.reshape(batch + (size, size))


def block_system(key_block, log_decay, beta_block):
    key_unit = key_block / jnp.sqrt(jnp.sum(key_block * key_block, axis=-1, keepdims=True) + 1e-06)
    cumulative = jnp.cumsum(log_decay, axis=-1)
    sequence_length = key_block.shape[1]
    lower_mask = jnp.tril(jnp.ones((sequence_length, sequence_length), dtype=jnp.bool_))
    strict = jnp.tril(jnp.ones((sequence_length, sequence_length), dtype=jnp.bool_), -1)
    spread = cumulative[:, :, None] - cumulative[:, None, :]
    ratios = jnp.where(lower_mask, jnp.exp(jnp.where(lower_mask, spread, 0.0)), 0.0)
    key_inner = matmul("bik,bjk->bij", key_unit, key_unit)
    system = jnp.where(strict, beta_block[:, :, None] * ratios * key_inner, 0.0) + jnp.eye(
        sequence_length, dtype=jnp.float32
    )
    return key_unit, cumulative, ratios, unit_lower_inverse(system)


def block_terms(query_block, key_block, value_block, log_decay, beta_block):
    key_unit, cumulative, ratios, system_inverse = block_system(key_block, log_decay, beta_block)
    growth = jnp.exp(cumulative)
    right_side = jnp.concatenate(
        [beta_block[:, :, None] * value_block, (beta_block * growth)[:, :, None] * key_unit],
        axis=-1,
    )
    solved = matmul("bij,bjv->biv", system_inverse, right_side)
    value_size = value_block.shape[-1]
    updates = solved[:, :, :value_size]
    weighted = solved[:, :, value_size:]
    attend = ratios * matmul("bik,bjk->bij", query_block, key_unit)
    local_out = matmul("bij,bjv->biv", attend, updates)
    state_query = growth[:, :, None] * query_block - matmul("bij,bjk->bik", attend, weighted)
    key_tail = jnp.exp(cumulative[:, -1:] - cumulative)[:, :, None] * key_unit
    return (local_out, state_query, key_tail, weighted, updates, growth[:, -1])


def column_operator(query_block, key_block, log_decay, beta_block):
    key_unit, cumulative, ratios, system_inverse = block_system(key_block, log_decay, beta_block)
    attend = ratios * matmul("bik,bjk->bij", query_block, key_unit)
    return matmul("bij,bjk->bik", attend, system_inverse) * beta_block[:, None, :]


def to_heads(array, leading_count, sequence_length, head_count, head_size):
    shaped = array.astype(jnp.float32).reshape(
        leading_count, sequence_length, head_count, head_size
    )
    return shaped.transpose(0, 2, 1, 3).reshape(
        leading_count * head_count, sequence_length, head_size
    )


def gates_to_heads(array, leading_count, sequence_length, head_count):
    return array.transpose(0, 2, 1).reshape(leading_count * head_count, sequence_length)


def from_heads(array, leading_count, sequence_length, head_count, head_size):
    return array.reshape(leading_count, head_count, sequence_length, head_size).transpose(
        0, 2, 1, 3
    )


def head_norm(array, gain):
    return array * lax.rsqrt(jnp.mean(array * array, axis=-1, keepdims=True) + 1e-05) * gain


def prefix_states(transfer, offset):
    scan_count = lax.axis_size("scan")
    head_size = offset.shape[-1]
    distance = 1
    while distance < scan_count:
        if 2 * distance < scan_count:
            arrived = from_behind(jnp.concatenate([transfer, offset], axis=-1), "scan", distance)
            composed = matmul("bij,bjv->biv", transfer, arrived)
            transfer = composed[:, :, :head_size]
            offset = composed[:, :, head_size:] + offset
        else:
            arrived = from_behind(offset, "scan", distance)
            offset = matmul("bij,bjv->biv", transfer, arrived) + offset
        distance *= 2
    return from_behind(offset, "scan", 1)


def shards(
    query_row,
    key_row,
    value_row,
    decay_row,
    beta_row,
    gain_row,
    query_col,
    key_col,
    decay_col,
    beta_col,
    gain_col,
):
    row_count, segment, features = query_row.shape
    head_size = gain_row.shape[0]
    head_count = features // head_size
    line_count = lax.axis_size("line")
    total_rows = query_col.shape[0]
    column_count = query_col.shape[2]

    def columns(array):
        return array.reshape(total_rows, column_count, -1).transpose(1, 0, 2)

    local_out, state_query, key_tail, weighted, updates, ending = block_terms(
        to_heads(query_row, row_count, segment, head_count, head_size),
        to_heads(key_row, row_count, segment, head_count, head_size),
        to_heads(value_row, row_count, segment, head_count, head_size),
        gates_to_heads(decay_row, row_count, segment, head_count),
        gates_to_heads(beta_row, row_count, segment, head_count),
    )
    identity = jnp.broadcast_to(
        jnp.eye(head_size, dtype=jnp.float32), (row_count * head_count, head_size, head_size)
    )
    transfer = ending[:, None, None] * identity - matmul("bjk,bjl->bkl", key_tail, weighted)
    offset = matmul("bjk,bjv->bkv", key_tail, updates)

    operator = column_operator(
        to_heads(columns(query_col), column_count, total_rows, head_count, head_size),
        to_heads(columns(key_col), column_count, total_rows, head_count, head_size),
        gates_to_heads(columns(decay_col), column_count, total_rows, head_count),
        gates_to_heads(columns(beta_col), column_count, total_rows, head_count),
    )

    incoming = prefix_states(transfer, offset)
    row_out = local_out + matmul("bik,bkv->biv", state_query, incoming)
    row_scan = from_heads(row_out, row_count, segment, head_count, head_size)
    values_col = (
        head_norm(row_scan, gain_row).reshape(row_count, segment, features).astype(jnp.bfloat16)
    )
    arranged = values_col.reshape(row_count, line_count, segment // line_count, features)
    column_values = lax.all_to_all(arranged, "line", split_axis=1, concat_axis=0, tiled=True)

    col_out = matmul(
        "bij,bjv->biv",
        operator,
        to_heads(columns(column_values), column_count, total_rows, head_count, head_size),
    )
    col_scan = from_heads(col_out, column_count, total_rows, head_count, head_size)
    normed = (
        head_norm(col_scan, gain_col)
        .transpose(1, 0, 2, 3)
        .reshape(total_rows, 1, column_count, features)
        .astype(jnp.bfloat16)
    )
    returned = lax.all_to_all(normed, "line", split_axis=0, concat_axis=1, tiled=True)
    return returned.reshape(row_count, segment, features)


def solution(mesh):
    placed = (
        P("line", "scan", None),
        P("line", "scan", None),
        P("line", "scan", None),
        P("line", "scan", None),
        P("line", "scan", None),
        P(),
        P(None, "scan", "line", None),
        P(None, "scan", "line", None),
        P(None, "scan", "line", None),
        P(None, "scan", "line", None),
        P(),
    )
    return jax.shard_map(
        shards, mesh=mesh, in_specs=placed, out_specs=P("line", "scan", None), check_vma=False
    )
```

```python
import jax
import jax.numpy as jnp
from jax import lax
from jax.sharding import PartitionSpec as P

HIGHEST = lax.Precision.HIGHEST
BASE_BLOCK = 16


def from_behind(block, axis, distance):
    devices = range(lax.axis_size(axis))
    route = [(i - distance, i) for i in devices if i - distance in devices]
    return lax.ppermute(block, axis, route)


def matmul(spec, left, right):
    return jnp.einsum(spec, left, right, precision=HIGHEST)


def unit_lower_inverse(system):
    size = system.shape[-1]
    base = min(BASE_BLOCK, size)
    assert size % base == 0
    rows = lax.broadcasted_iota(jnp.int32, (size, size), 0)
    cols = lax.broadcasted_iota(jnp.int32, (size, size), 1)
    eye = jnp.eye(size, dtype=jnp.float32)
    lower = system - eye
    diagonal = jnp.where(rows // base == cols // base, lower, 0.0)
    inverse = eye - diagonal
    power = diagonal
    reach = 2
    while reach < base:
        power = matmul("...ij,...jk->...ik", power, power)
        inverse = inverse + matmul("...ij,...jk->...ik", inverse, power)
        reach *= 2
    width = base
    while width < size:
        inside = (rows // (2 * width) == cols // (2 * width)) & (rows // width != cols // width)
        coupling = jnp.where(inside, lower, 0.0)
        inverse = inverse - matmul(
            "...ij,...jk->...ik", matmul("...ij,...jk->...ik", inverse, coupling), inverse
        )
        width *= 2
    return inverse


def block_system(key_block, log_decay, beta_block):
    key_unit = key_block / jnp.sqrt(jnp.sum(key_block * key_block, axis=-1, keepdims=True) + 1e-06)
    cumulative = jnp.cumsum(log_decay, axis=-1)
    sequence_length = key_block.shape[1]
    lower_mask = jnp.tril(jnp.ones((sequence_length, sequence_length), dtype=jnp.bool_))
    strict = jnp.tril(jnp.ones((sequence_length, sequence_length), dtype=jnp.bool_), -1)
    spread = cumulative[:, :, None] - cumulative[:, None, :]
    ratios = jnp.where(lower_mask, jnp.exp(jnp.where(lower_mask, spread, 0.0)), 0.0)
    key_inner = matmul("bik,bjk->bij", key_unit, key_unit)
    system = jnp.where(strict, beta_block[:, :, None] * ratios * key_inner, 0.0) + jnp.eye(
        sequence_length, dtype=jnp.float32
    )
    return key_unit, cumulative, ratios, unit_lower_inverse(system)


def block_terms(query_block, key_block, value_block, log_decay, beta_block):
    key_unit, cumulative, ratios, system_inverse = block_system(key_block, log_decay, beta_block)
    growth = jnp.exp(cumulative)
    right_side = jnp.concatenate(
        [beta_block[:, :, None] * value_block, (beta_block * growth)[:, :, None] * key_unit],
        axis=-1,
    )
    solved = matmul("bij,bjv->biv", system_inverse, right_side)
    value_size = value_block.shape[-1]
    updates = solved[:, :, :value_size]
    weighted = solved[:, :, value_size:]
    attend = ratios * matmul("bik,bjk->bij", query_block, key_unit)
    local_out = matmul("bij,bjv->biv", attend, updates)
    state_query = growth[:, :, None] * query_block - matmul("bij,bjk->bik", attend, weighted)
    key_tail = jnp.exp(cumulative[:, -1:] - cumulative)[:, :, None] * key_unit
    return (local_out, state_query, key_tail, weighted, updates, growth[:, -1])


def column_operator(query_block, key_block, log_decay, beta_block):
    key_unit, cumulative, ratios, system_inverse = block_system(key_block, log_decay, beta_block)
    attend = ratios * matmul("bik,bjk->bij", query_block, key_unit)
    return matmul("bij,bjk->bik", attend, system_inverse) * beta_block[:, None, :]


def to_heads(array, leading_count, sequence_length, head_count, head_size):
    shaped = array.astype(jnp.float32).reshape(
        leading_count, sequence_length, head_count, head_size
    )
    return shaped.transpose(0, 2, 1, 3).reshape(
        leading_count * head_count, sequence_length, head_size
    )


def gates_to_heads(array, leading_count, sequence_length, head_count):
    return array.transpose(0, 2, 1).reshape(leading_count * head_count, sequence_length)


def from_heads(array, leading_count, sequence_length, head_count, head_size):
    return array.reshape(leading_count, head_count, sequence_length, head_size).transpose(
        0, 2, 1, 3
    )


def head_norm(array, gain):
    return array * lax.rsqrt(jnp.mean(array * array, axis=-1, keepdims=True) + 1e-05) * gain


def prefix_states(transfer, offset):
    scan_count = lax.axis_size("scan")
    head_size = offset.shape[-1]
    distance = 1
    while distance < scan_count:
        if 2 * distance < scan_count:
            arrived = from_behind(jnp.concatenate([transfer, offset], axis=-1), "scan", distance)
            composed = matmul("bij,bjv->biv", transfer, arrived)
            transfer = composed[:, :, :head_size]
            offset = composed[:, :, head_size:] + offset
        else:
            arrived = from_behind(offset, "scan", distance)
            offset = matmul("bij,bjv->biv", transfer, arrived) + offset
        distance *= 2
    return from_behind(offset, "scan", 1)


def shards(
    query_row,
    key_row,
    value_row,
    decay_row,
    beta_row,
    gain_row,
    query_col,
    key_col,
    decay_col,
    beta_col,
    gain_col,
):
    row_count, segment, features = query_row.shape
    head_size = gain_row.shape[0]
    head_count = features // head_size
    line_count = lax.axis_size("z") * lax.axis_size("core")
    total_rows = query_col.shape[0]
    column_count = query_col.shape[2]

    def columns(array):
        return array.reshape(total_rows, column_count, -1).transpose(1, 0, 2)

    local_out, state_query, key_tail, weighted, updates, ending = block_terms(
        to_heads(query_row, row_count, segment, head_count, head_size),
        to_heads(key_row, row_count, segment, head_count, head_size),
        to_heads(value_row, row_count, segment, head_count, head_size),
        gates_to_heads(decay_row, row_count, segment, head_count),
        gates_to_heads(beta_row, row_count, segment, head_count),
    )
    identity = jnp.broadcast_to(
        jnp.eye(head_size, dtype=jnp.float32), (row_count * head_count, head_size, head_size)
    )
    transfer = ending[:, None, None] * identity - matmul("bjk,bjl->bkl", key_tail, weighted)
    offset = matmul("bjk,bjv->bkv", key_tail, updates)

    operator = column_operator(
        to_heads(columns(query_col), column_count, total_rows, head_count, head_size),
        to_heads(columns(key_col), column_count, total_rows, head_count, head_size),
        gates_to_heads(columns(decay_col), column_count, total_rows, head_count),
        gates_to_heads(columns(beta_col), column_count, total_rows, head_count),
    )

    incoming = prefix_states(transfer, offset)
    row_out = local_out + matmul("bik,bkv->biv", state_query, incoming)
    row_scan = from_heads(row_out, row_count, segment, head_count, head_size)
    values_col = (
        head_norm(row_scan, gain_row).reshape(row_count, segment, features).astype(jnp.bfloat16)
    )
    chip_count = lax.axis_size("z")
    core_count = lax.axis_size("core")
    arranged = values_col.reshape(
        row_count, chip_count, core_count, segment // line_count, features
    )
    by_chip = lax.all_to_all(arranged, "z", split_axis=1, concat_axis=0, tiled=True)
    by_core = lax.all_to_all(by_chip, "core", split_axis=2, concat_axis=1, tiled=True)
    column_values = by_core.reshape(total_rows, column_count, features)

    col_out = matmul(
        "bij,bjv->biv",
        operator,
        to_heads(columns(column_values), column_count, total_rows, head_count, head_size),
    )
    col_scan = from_heads(col_out, column_count, total_rows, head_count, head_size)
    normed = (
        head_norm(col_scan, gain_col)
        .transpose(1, 0, 2, 3)
        .reshape(chip_count, core_count, 1, column_count, features)
        .astype(jnp.bfloat16)
    )
    to_core = lax.all_to_all(normed, "core", split_axis=1, concat_axis=2, tiled=True)
    to_chip = lax.all_to_all(to_core, "z", split_axis=0, concat_axis=1, tiled=True)
    return to_chip.reshape(row_count, segment, features)


def solution(mesh):
    line_devices, scan_devices = mesh.devices.shape
    cores = 2 if line_devices % 2 == 0 else 1
    split = jax.sharding.Mesh(
        mesh.devices.reshape(line_devices // cores, cores, scan_devices), ("z", "core", "scan")
    )
    line = ("z", "core")
    placed = (
        P(line, "scan", None),
        P(line, "scan", None),
        P(line, "scan", None),
        P(line, "scan", None),
        P(line, "scan", None),
        P(),
        P(None, "scan", line, None),
        P(None, "scan", line, None),
        P(None, "scan", line, None),
        P(None, "scan", line, None),
        P(),
    )
    return jax.shard_map(
        shards, mesh=split, in_specs=placed, out_specs=P(line, "scan", None), check_vma=False
    )
```

```python
import jax
import jax.numpy as jnp
from jax import lax
from jax.sharding import PartitionSpec as P

HIGHEST = lax.Precision.HIGHEST
BASE_BLOCK = 16
INNER = ("near", "core")
LINE = ("outer",) + INNER


def from_behind(block, axis, distance):
    devices = range(lax.axis_size(axis))
    route = [(i - distance, i) for i in devices if i - distance in devices]
    return lax.ppermute(block, axis, route)


def matmul(spec, left, right):
    return jnp.einsum(spec, left, right, precision=HIGHEST)


def unit_lower_inverse(system):
    size = system.shape[-1]
    base = min(BASE_BLOCK, size)
    assert size % base == 0
    rows = lax.broadcasted_iota(jnp.int32, (size, size), 0)
    cols = lax.broadcasted_iota(jnp.int32, (size, size), 1)
    eye = jnp.eye(size, dtype=jnp.float32)
    lower = system - eye
    diagonal = jnp.where(rows // base == cols // base, lower, 0.0)
    inverse = eye - diagonal
    power = diagonal
    reach = 2
    while reach < base:
        power = matmul("...ij,...jk->...ik", power, power)
        inverse = inverse + matmul("...ij,...jk->...ik", inverse, power)
        reach *= 2
    width = base
    while width < size:
        inside = (rows // (2 * width) == cols // (2 * width)) & (rows // width != cols // width)
        coupling = jnp.where(inside, lower, 0.0)
        inverse = inverse - matmul(
            "...ij,...jk->...ik", matmul("...ij,...jk->...ik", inverse, coupling), inverse
        )
        width *= 2
    return inverse


def block_system(key_block, log_decay, beta_block):
    key_unit = key_block / jnp.sqrt(jnp.sum(key_block * key_block, axis=-1, keepdims=True) + 1e-06)
    cumulative = jnp.cumsum(log_decay, axis=-1)
    sequence_length = key_block.shape[1]
    lower_mask = jnp.tril(jnp.ones((sequence_length, sequence_length), dtype=jnp.bool_))
    strict = jnp.tril(jnp.ones((sequence_length, sequence_length), dtype=jnp.bool_), -1)
    spread = cumulative[:, :, None] - cumulative[:, None, :]
    ratios = jnp.where(lower_mask, jnp.exp(jnp.where(lower_mask, spread, 0.0)), 0.0)
    key_inner = matmul("bik,bjk->bij", key_unit, key_unit)
    system = jnp.where(strict, beta_block[:, :, None] * ratios * key_inner, 0.0) + jnp.eye(
        sequence_length, dtype=jnp.float32
    )
    return key_unit, cumulative, ratios, unit_lower_inverse(system)


def block_terms(query_block, key_block, value_block, log_decay, beta_block):
    key_unit, cumulative, ratios, system_inverse = block_system(key_block, log_decay, beta_block)
    growth = jnp.exp(cumulative)
    right_side = jnp.concatenate(
        [beta_block[:, :, None] * value_block, (beta_block * growth)[:, :, None] * key_unit],
        axis=-1,
    )
    solved = matmul("bij,bjv->biv", system_inverse, right_side)
    value_size = value_block.shape[-1]
    updates = solved[:, :, :value_size]
    weighted = solved[:, :, value_size:]
    attend = ratios * matmul("bik,bjk->bij", query_block, key_unit)
    local_out = matmul("bij,bjv->biv", attend, updates)
    state_query = growth[:, :, None] * query_block - matmul("bij,bjk->bik", attend, weighted)
    key_tail = jnp.exp(cumulative[:, -1:] - cumulative)[:, :, None] * key_unit
    return (local_out, state_query, key_tail, weighted, updates, growth[:, -1])


def column_operator(query_block, key_block, log_decay, beta_block):
    key_unit, cumulative, ratios, system_inverse = block_system(key_block, log_decay, beta_block)
    attend = ratios * matmul("bik,bjk->bij", query_block, key_unit)
    return matmul("bij,bjk->bik", attend, system_inverse) * beta_block[:, None, :]


def to_heads(array, leading_count, sequence_length, head_count, head_size):
    shaped = array.astype(jnp.float32).reshape(
        leading_count, sequence_length, head_count, head_size
    )
    return shaped.transpose(0, 2, 1, 3).reshape(
        leading_count * head_count, sequence_length, head_size
    )


def gates_to_heads(array, leading_count, sequence_length, head_count):
    return array.transpose(0, 2, 1).reshape(leading_count * head_count, sequence_length)


def from_heads(array, leading_count, sequence_length, head_count, head_size):
    return array.reshape(leading_count, head_count, sequence_length, head_size).transpose(
        0, 2, 1, 3
    )


def head_norm(array, gain):
    return array * lax.rsqrt(jnp.mean(array * array, axis=-1, keepdims=True) + 1e-05) * gain


def prefix_states(transfer, offset):
    scan_count = lax.axis_size("scan")
    head_size = offset.shape[-1]
    distance = 1
    while distance < scan_count:
        if 2 * distance < scan_count:
            arrived = from_behind(jnp.concatenate([transfer, offset], axis=-1), "scan", distance)
            composed = matmul("bij,bjv->biv", transfer, arrived)
            transfer = composed[:, :, :head_size]
            offset = composed[:, :, head_size:] + offset
        else:
            arrived = from_behind(offset, "scan", distance)
            offset = matmul("bij,bjv->biv", transfer, arrived) + offset
        distance *= 2
    return from_behind(offset, "scan", 1)


def shards(
    query_row,
    key_row,
    value_row,
    decay_row,
    beta_row,
    gain_row,
    query_col,
    key_col,
    decay_col,
    beta_col,
    gain_col,
):
    row_count, segment, features = query_row.shape
    head_size = gain_row.shape[0]
    head_count = features // head_size
    line_count = lax.axis_size(LINE)
    total_rows = query_col.shape[0]
    column_count = query_col.shape[2]

    def columns(array):
        return array.reshape(total_rows, column_count, -1).transpose(1, 0, 2)

    local_out, state_query, key_tail, weighted, updates, ending = block_terms(
        to_heads(query_row, row_count, segment, head_count, head_size),
        to_heads(key_row, row_count, segment, head_count, head_size),
        to_heads(value_row, row_count, segment, head_count, head_size),
        gates_to_heads(decay_row, row_count, segment, head_count),
        gates_to_heads(beta_row, row_count, segment, head_count),
    )
    identity = jnp.broadcast_to(
        jnp.eye(head_size, dtype=jnp.float32), (row_count * head_count, head_size, head_size)
    )
    transfer = ending[:, None, None] * identity - matmul("bjk,bjl->bkl", key_tail, weighted)
    offset = matmul("bjk,bjv->bkv", key_tail, updates)

    operator = column_operator(
        to_heads(columns(query_col), column_count, total_rows, head_count, head_size),
        to_heads(columns(key_col), column_count, total_rows, head_count, head_size),
        gates_to_heads(columns(decay_col), column_count, total_rows, head_count),
        gates_to_heads(columns(beta_col), column_count, total_rows, head_count),
    )

    incoming = prefix_states(transfer, offset)
    row_out = local_out + matmul("bik,bkv->biv", state_query, incoming)
    row_scan = from_heads(row_out, row_count, segment, head_count, head_size)
    values_col = (
        head_norm(row_scan, gain_row).reshape(row_count, segment, features).astype(jnp.bfloat16)
    )
    outer_count = lax.axis_size("outer")
    inner_count = lax.axis_size(INNER)
    arranged = values_col.reshape(
        1, 1, outer_count, inner_count, segment // line_count, features
    )
    by_inner = lax.all_to_all(arranged, INNER, split_axis=3, concat_axis=1, tiled=True)
    by_outer = lax.all_to_all(by_inner, "outer", split_axis=2, concat_axis=0, tiled=True)
    column_values = by_outer.reshape(total_rows, column_count, features)

    col_out = matmul(
        "bij,bjv->biv",
        operator,
        to_heads(columns(column_values), column_count, total_rows, head_count, head_size),
    )
    col_scan = from_heads(col_out, column_count, total_rows, head_count, head_size)
    normed = (
        head_norm(col_scan, gain_col)
        .transpose(1, 0, 2, 3)
        .reshape(outer_count, inner_count, 1, 1, column_count, features)
        .astype(jnp.bfloat16)
    )
    to_inner = lax.all_to_all(normed, INNER, split_axis=1, concat_axis=3, tiled=True)
    to_outer = lax.all_to_all(to_inner, "outer", split_axis=0, concat_axis=2, tiled=True)
    return to_outer.reshape(row_count, segment, features)


def solution(mesh):
    line_devices, scan_devices = mesh.devices.shape
    cores = 2 if line_devices % 2 == 0 else 1
    chips = line_devices // cores
    near = 4 if chips % 4 == 0 else 1
    split = jax.sharding.Mesh(
        mesh.devices.reshape(chips // near, near, cores, scan_devices),
        ("outer", "near", "core", "scan"),
    )
    placed = (
        P(LINE, "scan", None),
        P(LINE, "scan", None),
        P(LINE, "scan", None),
        P(LINE, "scan", None),
        P(LINE, "scan", None),
        P(),
        P(None, "scan", LINE, None),
        P(None, "scan", LINE, None),
        P(None, "scan", LINE, None),
        P(None, "scan", LINE, None),
        P(),
    )
    return jax.shard_map(
        shards, mesh=split, in_specs=placed, out_specs=P(LINE, "scan", None), check_vma=False
    )
```

```python
import jax
import jax.numpy as jnp
from jax import lax
from jax.sharding import PartitionSpec as P

HIGHEST = lax.Precision.HIGHEST
BASE_BLOCK = 16


def from_behind(block, axis, distance):
    devices = range(lax.axis_size(axis))
    route = [(i - distance, i) for i in devices if i - distance in devices]
    return lax.ppermute(block, axis, route)


def matmul(spec, left, right):
    return jnp.einsum(spec, left, right, precision=HIGHEST)


def unit_lower_inverse(system):
    size = system.shape[-1]
    base = min(BASE_BLOCK, size)
    assert size % base == 0
    rows = lax.broadcasted_iota(jnp.int32, (size, size), 0)
    cols = lax.broadcasted_iota(jnp.int32, (size, size), 1)
    eye = jnp.eye(size, dtype=jnp.float32)
    lower = system - eye
    diagonal = jnp.where(rows // base == cols // base, lower, 0.0)
    inverse = eye - diagonal
    power = diagonal
    reach = 2
    while reach < base:
        power = matmul("...ij,...jk->...ik", power, power)
        inverse = inverse + matmul("...ij,...jk->...ik", inverse, power)
        reach *= 2
    width = base
    while width < size:
        inside = (rows // (2 * width) == cols // (2 * width)) & (rows // width != cols // width)
        coupling = jnp.where(inside, lower, 0.0)
        inverse = inverse - matmul(
            "...ij,...jk->...ik", matmul("...ij,...jk->...ik", inverse, coupling), inverse
        )
        width *= 2
    return inverse


def block_system(key_block, log_decay, beta_block):
    key_unit = key_block / jnp.sqrt(jnp.sum(key_block * key_block, axis=-1, keepdims=True) + 1e-06)
    cumulative = jnp.cumsum(log_decay, axis=-1)
    sequence_length = key_block.shape[1]
    lower_mask = jnp.tril(jnp.ones((sequence_length, sequence_length), dtype=jnp.bool_))
    strict = jnp.tril(jnp.ones((sequence_length, sequence_length), dtype=jnp.bool_), -1)
    spread = cumulative[:, :, None] - cumulative[:, None, :]
    ratios = jnp.where(lower_mask, jnp.exp(jnp.where(lower_mask, spread, 0.0)), 0.0)
    key_inner = matmul("bik,bjk->bij", key_unit, key_unit)
    system = jnp.where(strict, beta_block[:, :, None] * ratios * key_inner, 0.0) + jnp.eye(
        sequence_length, dtype=jnp.float32
    )
    return key_unit, cumulative, ratios, unit_lower_inverse(system)


def block_terms(query_block, key_block, value_block, log_decay, beta_block):
    key_unit, cumulative, ratios, system_inverse = block_system(key_block, log_decay, beta_block)
    growth = jnp.exp(cumulative)
    right_side = jnp.concatenate(
        [beta_block[:, :, None] * value_block, (beta_block * growth)[:, :, None] * key_unit],
        axis=-1,
    )
    solved = matmul("bij,bjv->biv", system_inverse, right_side)
    value_size = value_block.shape[-1]
    updates = solved[:, :, :value_size]
    weighted = solved[:, :, value_size:]
    attend = ratios * matmul("bik,bjk->bij", query_block, key_unit)
    local_out = matmul("bij,bjv->biv", attend, updates)
    state_query = growth[:, :, None] * query_block - matmul("bij,bjk->bik", attend, weighted)
    key_tail = jnp.exp(cumulative[:, -1:] - cumulative)[:, :, None] * key_unit
    return (local_out, state_query, key_tail, weighted, updates, growth[:, -1])


def column_operator(query_block, key_block, log_decay, beta_block):
    key_unit, cumulative, ratios, system_inverse = block_system(key_block, log_decay, beta_block)
    attend = ratios * matmul("bik,bjk->bij", query_block, key_unit)
    return matmul("bij,bjk->bik", attend, system_inverse) * beta_block[:, None, :]


def to_heads(array, leading_count, sequence_length, head_count, head_size):
    shaped = array.astype(jnp.float32).reshape(
        leading_count, sequence_length, head_count, head_size
    )
    return shaped.transpose(0, 2, 1, 3).reshape(
        leading_count * head_count, sequence_length, head_size
    )


def gates_to_heads(array, leading_count, sequence_length, head_count):
    return array.transpose(0, 2, 1).reshape(leading_count * head_count, sequence_length)


def from_heads(array, leading_count, sequence_length, head_count, head_size):
    return array.reshape(leading_count, head_count, sequence_length, head_size).transpose(
        0, 2, 1, 3
    )


def head_norm(array, gain):
    return array * lax.rsqrt(jnp.mean(array * array, axis=-1, keepdims=True) + 1e-05) * gain


def prefix_states(transfer, offset):
    scan_count = lax.axis_size("scan")
    distance = 1
    while distance < scan_count:
        if 2 * distance < scan_count:
            sent_transfer, arrived = from_behind(
                (transfer.astype(jnp.bfloat16), offset), "scan", distance
            )
            offset = matmul("bij,bjv->biv", transfer, arrived) + offset
            transfer = matmul("bij,bjv->biv", transfer, sent_transfer.astype(jnp.float32))
        else:
            arrived = from_behind(offset, "scan", distance)
            offset = matmul("bij,bjv->biv", transfer, arrived) + offset
        distance *= 2
    return from_behind(offset, "scan", 1)


def shards(
    query_row,
    key_row,
    value_row,
    decay_row,
    beta_row,
    gain_row,
    query_col,
    key_col,
    decay_col,
    beta_col,
    gain_col,
):
    row_count, segment, features = query_row.shape
    head_size = gain_row.shape[0]
    head_count = features // head_size
    line_count = lax.axis_size("line")
    total_rows = query_col.shape[0]
    column_count = query_col.shape[2]

    def columns(array):
        return array.reshape(total_rows, column_count, -1).transpose(1, 0, 2)

    local_out, state_query, key_tail, weighted, updates, ending = block_terms(
        to_heads(query_row, row_count, segment, head_count, head_size),
        to_heads(key_row, row_count, segment, head_count, head_size),
        to_heads(value_row, row_count, segment, head_count, head_size),
        gates_to_heads(decay_row, row_count, segment, head_count),
        gates_to_heads(beta_row, row_count, segment, head_count),
    )
    identity = jnp.broadcast_to(
        jnp.eye(head_size, dtype=jnp.float32), (row_count * head_count, head_size, head_size)
    )
    transfer = ending[:, None, None] * identity - matmul("bjk,bjl->bkl", key_tail, weighted)
    offset = matmul("bjk,bjv->bkv", key_tail, updates)

    operator = column_operator(
        to_heads(columns(query_col), column_count, total_rows, head_count, head_size),
        to_heads(columns(key_col), column_count, total_rows, head_count, head_size),
        gates_to_heads(columns(decay_col), column_count, total_rows, head_count),
        gates_to_heads(columns(beta_col), column_count, total_rows, head_count),
    )

    incoming = prefix_states(transfer, offset)
    row_out = local_out + matmul("bik,bkv->biv", state_query, incoming)
    row_scan = from_heads(row_out, row_count, segment, head_count, head_size)
    values_col = (
        head_norm(row_scan, gain_row).reshape(row_count, segment, features).astype(jnp.bfloat16)
    )
    values_col, operator = lax.optimization_barrier((values_col, operator))
    arranged = values_col.reshape(row_count, line_count, segment // line_count, features)
    column_values = lax.all_to_all(arranged, "line", split_axis=1, concat_axis=0, tiled=True)

    col_out = matmul(
        "bij,bjv->biv",
        operator,
        to_heads(columns(column_values), column_count, total_rows, head_count, head_size),
    )
    col_scan = from_heads(col_out, column_count, total_rows, head_count, head_size)
    normed = (
        head_norm(col_scan, gain_col)
        .transpose(1, 0, 2, 3)
        .reshape(total_rows, 1, column_count, features)
        .astype(jnp.bfloat16)
    )
    returned = lax.all_to_all(normed, "line", split_axis=0, concat_axis=1, tiled=True)
    return returned.reshape(row_count, segment, features)


def solution(mesh):
    placed = (
        P("line", "scan", None),
        P("line", "scan", None),
        P("line", "scan", None),
        P("line", "scan", None),
        P("line", "scan", None),
        P(),
        P(None, "scan", "line", None),
        P(None, "scan", "line", None),
        P(None, "scan", "line", None),
        P(None, "scan", "line", None),
        P(),
    )
    return jax.shard_map(
        shards, mesh=mesh, in_specs=placed, out_specs=P("line", "scan", None), check_vma=False
    )
```

```python
import jax
import jax.numpy as jnp
from jax import lax
from jax.sharding import PartitionSpec as P

HIGHEST = lax.Precision.HIGHEST
BASE_BLOCK = 16


def from_behind(block, axis, distance):
    devices = range(lax.axis_size(axis))
    route = [(i - distance, i) for i in devices if i - distance in devices]
    return lax.ppermute(block, axis, route)


def matmul(spec, left, right):
    return jnp.einsum(spec, left, right, precision=HIGHEST)


def unit_lower_inverse(system):
    size = system.shape[-1]
    base = min(BASE_BLOCK, size)
    assert size % base == 0
    rows = lax.broadcasted_iota(jnp.int32, (size, size), 0)
    cols = lax.broadcasted_iota(jnp.int32, (size, size), 1)
    eye = jnp.eye(size, dtype=jnp.float32)
    lower = system - eye
    diagonal = jnp.where(rows // base == cols // base, lower, 0.0)
    inverse = eye - diagonal
    power = diagonal
    reach = 2
    while reach < base:
        power = matmul("...ij,...jk->...ik", power, power)
        inverse = inverse + matmul("...ij,...jk->...ik", inverse, power)
        reach *= 2
    width = base
    while width < size:
        inside = (rows // (2 * width) == cols // (2 * width)) & (rows // width != cols // width)
        coupling = jnp.where(inside, lower, 0.0)
        inverse = inverse - matmul(
            "...ij,...jk->...ik", matmul("...ij,...jk->...ik", inverse, coupling), inverse
        )
        width *= 2
    return inverse


def block_system(key_block, log_decay, beta_block):
    key_unit = key_block / jnp.sqrt(jnp.sum(key_block * key_block, axis=-1, keepdims=True) + 1e-06)
    cumulative = jnp.cumsum(log_decay, axis=-1)
    sequence_length = key_block.shape[1]
    lower_mask = jnp.tril(jnp.ones((sequence_length, sequence_length), dtype=jnp.bool_))
    strict = jnp.tril(jnp.ones((sequence_length, sequence_length), dtype=jnp.bool_), -1)
    spread = cumulative[:, :, None] - cumulative[:, None, :]
    ratios = jnp.where(lower_mask, jnp.exp(jnp.where(lower_mask, spread, 0.0)), 0.0)
    key_inner = matmul("bik,bjk->bij", key_unit, key_unit)
    system = jnp.where(strict, beta_block[:, :, None] * ratios * key_inner, 0.0) + jnp.eye(
        sequence_length, dtype=jnp.float32
    )
    return key_unit, cumulative, ratios, unit_lower_inverse(system)


def block_terms(query_block, key_block, value_block, log_decay, beta_block):
    key_unit, cumulative, ratios, system_inverse = block_system(key_block, log_decay, beta_block)
    growth = jnp.exp(cumulative)
    right_side = jnp.concatenate(
        [beta_block[:, :, None] * value_block, (beta_block * growth)[:, :, None] * key_unit],
        axis=-1,
    )
    solved = matmul("bij,bjv->biv", system_inverse, right_side)
    value_size = value_block.shape[-1]
    updates = solved[:, :, :value_size]
    weighted = solved[:, :, value_size:]
    attend = ratios * matmul("bik,bjk->bij", query_block, key_unit)
    local_out = matmul("bij,bjv->biv", attend, updates)
    state_query = growth[:, :, None] * query_block - matmul("bij,bjk->bik", attend, weighted)
    key_tail = jnp.exp(cumulative[:, -1:] - cumulative)[:, :, None] * key_unit
    return (local_out, state_query, key_tail, weighted, updates, growth[:, -1])


def column_operator(query_block, key_block, log_decay, beta_block):
    key_unit, cumulative, ratios, system_inverse = block_system(key_block, log_decay, beta_block)
    attend = ratios * matmul("bik,bjk->bij", query_block, key_unit)
    return matmul("bij,bjk->bik", attend, system_inverse) * beta_block[:, None, :]


def to_heads(array, leading_count, sequence_length, head_count, head_size):
    shaped = array.astype(jnp.float32).reshape(
        leading_count, sequence_length, head_count, head_size
    )
    return shaped.transpose(0, 2, 1, 3).reshape(
        leading_count * head_count, sequence_length, head_size
    )


def gates_to_heads(array, leading_count, sequence_length, head_count):
    return array.transpose(0, 2, 1).reshape(leading_count * head_count, sequence_length)


def from_heads(array, leading_count, sequence_length, head_count, head_size):
    return array.reshape(leading_count, head_count, sequence_length, head_size).transpose(
        0, 2, 1, 3
    )


def head_norm(array, gain):
    return array * lax.rsqrt(jnp.mean(array * array, axis=-1, keepdims=True) + 1e-05) * gain


def prefix_states(transfer, offset):
    scan_count = lax.axis_size("scan")
    head_size = offset.shape[-1]
    ahead_transfer = jnp.zeros_like(transfer)
    ahead_offset = jnp.zeros_like(offset)
    distance = 1
    while distance < scan_count:
        if 2 * distance < scan_count:
            arrived = from_behind(jnp.concatenate([transfer, offset], axis=-1), "scan", distance)
            composed = matmul("bij,bjv->biv", transfer, arrived)
            if distance == 1:
                ahead_transfer = arrived[:, :, :head_size]
                ahead_offset = arrived[:, :, head_size:]
            else:
                ahead = matmul("bij,bjv->biv", ahead_transfer, arrived)
                ahead_transfer = ahead[:, :, :head_size]
                ahead_offset = ahead[:, :, head_size:] + ahead_offset
            transfer = composed[:, :, :head_size]
            offset = composed[:, :, head_size:] + offset
        else:
            arrived = from_behind(offset, "scan", distance)
            if distance == 1:
                ahead_offset = arrived
            else:
                ahead_offset = matmul("bij,bjv->biv", ahead_transfer, arrived) + ahead_offset
        distance *= 2
    return ahead_offset


def shards(
    query_row,
    key_row,
    value_row,
    decay_row,
    beta_row,
    gain_row,
    query_col,
    key_col,
    decay_col,
    beta_col,
    gain_col,
):
    row_count, segment, features = query_row.shape
    head_size = gain_row.shape[0]
    head_count = features // head_size
    line_count = lax.axis_size("line")
    total_rows = query_col.shape[0]
    column_count = query_col.shape[2]

    def columns(array):
        return array.reshape(total_rows, column_count, -1).transpose(1, 0, 2)

    local_out, state_query, key_tail, weighted, updates, ending = block_terms(
        to_heads(query_row, row_count, segment, head_count, head_size),
        to_heads(key_row, row_count, segment, head_count, head_size),
        to_heads(value_row, row_count, segment, head_count, head_size),
        gates_to_heads(decay_row, row_count, segment, head_count),
        gates_to_heads(beta_row, row_count, segment, head_count),
    )
    identity = jnp.broadcast_to(
        jnp.eye(head_size, dtype=jnp.float32), (row_count * head_count, head_size, head_size)
    )
    transfer = ending[:, None, None] * identity - matmul("bjk,bjl->bkl", key_tail, weighted)
    offset = matmul("bjk,bjv->bkv", key_tail, updates)

    operator = column_operator(
        to_heads(columns(query_col), column_count, total_rows, head_count, head_size),
        to_heads(columns(key_col), column_count, total_rows, head_count, head_size),
        gates_to_heads(columns(decay_col), column_count, total_rows, head_count),
        gates_to_heads(columns(beta_col), column_count, total_rows, head_count),
    )

    incoming = prefix_states(transfer, offset)
    row_out = local_out + matmul("bik,bkv->biv", state_query, incoming)
    row_scan = from_heads(row_out, row_count, segment, head_count, head_size)
    values_col = (
        head_norm(row_scan, gain_row).reshape(row_count, segment, features).astype(jnp.bfloat16)
    )
    values_col, operator = lax.optimization_barrier((values_col, operator))
    arranged = values_col.reshape(row_count, line_count, segment // line_count, features)
    column_values = lax.all_to_all(arranged, "line", split_axis=1, concat_axis=0, tiled=True)

    col_out = matmul(
        "bij,bjv->biv",
        operator,
        to_heads(columns(column_values), column_count, total_rows, head_count, head_size),
    )
    col_scan = from_heads(col_out, column_count, total_rows, head_count, head_size)
    normed = (
        head_norm(col_scan, gain_col)
        .transpose(1, 0, 2, 3)
        .reshape(total_rows, 1, column_count, features)
        .astype(jnp.bfloat16)
    )
    returned = lax.all_to_all(normed, "line", split_axis=0, concat_axis=1, tiled=True)
    return returned.reshape(row_count, segment, features)


def solution(mesh):
    placed = (
        P("line", "scan", None),
        P("line", "scan", None),
        P("line", "scan", None),
        P("line", "scan", None),
        P("line", "scan", None),
        P(),
        P(None, "scan", "line", None),
        P(None, "scan", "line", None),
        P(None, "scan", "line", None),
        P(None, "scan", "line", None),
        P(),
    )
    return jax.shard_map(
        shards, mesh=mesh, in_specs=placed, out_specs=P("line", "scan", None), check_vma=False
    )
```

```python
import jax
import jax.numpy as jnp
from jax import lax
from jax.sharding import PartitionSpec as P

HIGHEST = lax.Precision.HIGHEST
BASE_BLOCK = 16


def from_behind(block, axis, distance):
    devices = range(lax.axis_size(axis))
    route = [(i - distance, i) for i in devices if i - distance in devices]
    return lax.ppermute(block, axis, route)


def matmul(spec, left, right):
    return jnp.einsum(spec, left, right, precision=HIGHEST)


def unit_lower_inverse(system):
    size = system.shape[-1]
    base = min(BASE_BLOCK, size)
    assert size % base == 0
    rows = lax.broadcasted_iota(jnp.int32, (size, size), 0)
    cols = lax.broadcasted_iota(jnp.int32, (size, size), 1)
    eye = jnp.eye(size, dtype=jnp.float32)
    lower = system - eye
    diagonal = jnp.where(rows // base == cols // base, lower, 0.0)
    inverse = eye - diagonal
    power = diagonal
    reach = 2
    while reach < base:
        power = matmul("...ij,...jk->...ik", power, power)
        inverse = inverse + matmul("...ij,...jk->...ik", inverse, power)
        reach *= 2
    width = base
    while width < size:
        inside = (rows // (2 * width) == cols // (2 * width)) & (rows // width != cols // width)
        coupling = jnp.where(inside, lower, 0.0)
        inverse = inverse - matmul(
            "...ij,...jk->...ik", matmul("...ij,...jk->...ik", inverse, coupling), inverse
        )
        width *= 2
    return inverse


def block_system(key_block, log_decay, beta_block):
    key_unit = key_block / jnp.sqrt(jnp.sum(key_block * key_block, axis=-1, keepdims=True) + 1e-06)
    cumulative = jnp.cumsum(log_decay, axis=-1)
    sequence_length = key_block.shape[1]
    lower_mask = jnp.tril(jnp.ones((sequence_length, sequence_length), dtype=jnp.bool_))
    strict = jnp.tril(jnp.ones((sequence_length, sequence_length), dtype=jnp.bool_), -1)
    spread = cumulative[:, :, None] - cumulative[:, None, :]
    ratios = jnp.where(lower_mask, jnp.exp(jnp.where(lower_mask, spread, 0.0)), 0.0)
    key_inner = matmul("bik,bjk->bij", key_unit, key_unit)
    system = jnp.where(strict, beta_block[:, :, None] * ratios * key_inner, 0.0) + jnp.eye(
        sequence_length, dtype=jnp.float32
    )
    return key_unit, cumulative, ratios, unit_lower_inverse(system)


def block_terms(query_block, key_block, value_block, log_decay, beta_block):
    key_unit, cumulative, ratios, system_inverse = block_system(key_block, log_decay, beta_block)
    growth = jnp.exp(cumulative)
    right_side = jnp.concatenate(
        [beta_block[:, :, None] * value_block, (beta_block * growth)[:, :, None] * key_unit],
        axis=-1,
    )
    solved = matmul("bij,bjv->biv", system_inverse, right_side)
    value_size = value_block.shape[-1]
    updates = solved[:, :, :value_size]
    weighted = solved[:, :, value_size:]
    attend = ratios * matmul("bik,bjk->bij", query_block, key_unit)
    local_out = matmul("bij,bjv->biv", attend, updates)
    state_query = growth[:, :, None] * query_block - matmul("bij,bjk->bik", attend, weighted)
    key_tail = jnp.exp(cumulative[:, -1:] - cumulative)[:, :, None] * key_unit
    return (local_out, state_query, key_tail, weighted, updates, growth[:, -1])


def column_operator(query_block, key_block, log_decay, beta_block):
    key_unit, cumulative, ratios, system_inverse = block_system(key_block, log_decay, beta_block)
    attend = ratios * matmul("bik,bjk->bij", query_block, key_unit)
    return matmul("bij,bjk->bik", attend, system_inverse) * beta_block[:, None, :]


def to_heads(array, leading_count, sequence_length, head_count, head_size):
    shaped = array.astype(jnp.float32).reshape(
        leading_count, sequence_length, head_count, head_size
    )
    return shaped.transpose(0, 2, 1, 3).reshape(
        leading_count * head_count, sequence_length, head_size
    )


def gates_to_heads(array, leading_count, sequence_length, head_count):
    return array.transpose(0, 2, 1).reshape(leading_count * head_count, sequence_length)


def from_heads(array, leading_count, sequence_length, head_count, head_size):
    return array.reshape(leading_count, head_count, sequence_length, head_size).transpose(
        0, 2, 1, 3
    )


def head_norm(array, gain):
    return array * lax.rsqrt(jnp.mean(array * array, axis=-1, keepdims=True) + 1e-05) * gain


def prefix_states(transfer, offset, fillers):
    scan_count = lax.axis_size("scan")
    head_size = offset.shape[-1]
    ahead_transfer = jnp.zeros_like(transfer)
    ahead_offset = jnp.zeros_like(offset)
    filled = []
    distance = 1
    while distance < scan_count:
        if 2 * distance < scan_count:
            arrived = from_behind(jnp.concatenate([transfer, offset], axis=-1), "scan", distance)
            if len(filled) < len(fillers):
                work, inputs = fillers[len(filled)]
                inputs, arrived = lax.optimization_barrier((inputs, arrived))
                filled.append(work(*inputs))
            composed = matmul("bij,bjv->biv", transfer, arrived)
            if distance == 1:
                ahead_transfer = arrived[:, :, :head_size]
                ahead_offset = arrived[:, :, head_size:]
            else:
                ahead = matmul("bij,bjv->biv", ahead_transfer, arrived)
                ahead_transfer = ahead[:, :, :head_size]
                ahead_offset = ahead[:, :, head_size:] + ahead_offset
            transfer = composed[:, :, :head_size]
            offset = composed[:, :, head_size:] + offset
        else:
            arrived = from_behind(offset, "scan", distance)
            if distance == 1:
                ahead_offset = arrived
            else:
                ahead_offset = matmul("bij,bjv->biv", ahead_transfer, arrived) + ahead_offset
        distance *= 2
    filled += [work(*inputs) for work, inputs in fillers[len(filled):]]
    return ahead_offset, filled


def shards(
    query_row,
    key_row,
    value_row,
    decay_row,
    beta_row,
    gain_row,
    query_col,
    key_col,
    decay_col,
    beta_col,
    gain_col,
):
    row_count, segment, features = query_row.shape
    head_size = gain_row.shape[0]
    head_count = features // head_size
    line_count = lax.axis_size("line")
    total_rows = query_col.shape[0]
    column_count = query_col.shape[2]

    def columns(array):
        return array.reshape(total_rows, column_count, -1).transpose(1, 0, 2)

    local_out, state_query, key_tail, weighted, updates, ending = block_terms(
        to_heads(query_row, row_count, segment, head_count, head_size),
        to_heads(key_row, row_count, segment, head_count, head_size),
        to_heads(value_row, row_count, segment, head_count, head_size),
        gates_to_heads(decay_row, row_count, segment, head_count),
        gates_to_heads(beta_row, row_count, segment, head_count),
    )
    identity = jnp.broadcast_to(
        jnp.eye(head_size, dtype=jnp.float32), (row_count * head_count, head_size, head_size)
    )
    transfer = ending[:, None, None] * identity - matmul("bjk,bjl->bkl", key_tail, weighted)
    offset = matmul("bjk,bjv->bkv", key_tail, updates)

    def column_part(query_part, key_part, decay_part, beta_part):
        def part_columns(array):
            return array.reshape(total_rows, query_part.shape[2], -1).transpose(1, 0, 2)

        count = query_part.shape[2]
        return column_operator(
            to_heads(part_columns(query_part), count, total_rows, head_count, head_size),
            to_heads(part_columns(key_part), count, total_rows, head_count, head_size),
            gates_to_heads(part_columns(decay_part), count, total_rows, head_count),
            gates_to_heads(part_columns(beta_part), count, total_rows, head_count),
        )

    column_inputs = (query_col, key_col, decay_col, beta_col)
    half = column_count // 2 if column_count % 2 == 0 else column_count
    fillers = [(column_part, tuple(piece[:, :, :half] for piece in column_inputs))]
    if half < column_count:
        fillers.append((column_part, tuple(piece[:, :, half:] for piece in column_inputs)))
    incoming, operators = prefix_states(transfer, offset, fillers)
    operator = jnp.concatenate(operators, axis=0)
    row_out = local_out + matmul("bik,bkv->biv", state_query, incoming)
    row_scan = from_heads(row_out, row_count, segment, head_count, head_size)
    values_col = (
        head_norm(row_scan, gain_row).reshape(row_count, segment, features).astype(jnp.bfloat16)
    )
    values_col, operator = lax.optimization_barrier((values_col, operator))
    arranged = values_col.reshape(row_count, line_count, segment // line_count, features)
    column_values = lax.all_to_all(arranged, "line", split_axis=1, concat_axis=0, tiled=True)

    col_out = matmul(
        "bij,bjv->biv",
        operator,
        to_heads(columns(column_values), column_count, total_rows, head_count, head_size),
    )
    col_scan = from_heads(col_out, column_count, total_rows, head_count, head_size)
    normed = (
        head_norm(col_scan, gain_col)
        .transpose(1, 0, 2, 3)
        .reshape(total_rows, 1, column_count, features)
        .astype(jnp.bfloat16)
    )
    returned = lax.all_to_all(normed, "line", split_axis=0, concat_axis=1, tiled=True)
    return returned.reshape(row_count, segment, features)


def solution(mesh):
    placed = (
        P("line", "scan", None),
        P("line", "scan", None),
        P("line", "scan", None),
        P("line", "scan", None),
        P("line", "scan", None),
        P(),
        P(None, "scan", "line", None),
        P(None, "scan", "line", None),
        P(None, "scan", "line", None),
        P(None, "scan", "line", None),
        P(),
    )
    return jax.shard_map(
        shards, mesh=mesh, in_specs=placed, out_specs=P("line", "scan", None), check_vma=False
    )
```

```python
import jax
import jax.numpy as jnp
from jax import lax
from jax.sharding import PartitionSpec as P

HIGHEST = lax.Precision.HIGHEST
BASE_BLOCK = 16


def from_behind(block, axis, distance):
    devices = range(lax.axis_size(axis))
    route = [(i - distance, i) for i in devices if i - distance in devices]
    return lax.ppermute(block, axis, route)


def matmul(spec, left, right):
    return jnp.einsum(spec, left, right, precision=HIGHEST)


def unit_lower_inverse(system):
    size = system.shape[-1]
    base = min(BASE_BLOCK, size)
    assert size % base == 0
    rows = lax.broadcasted_iota(jnp.int32, (size, size), 0)
    cols = lax.broadcasted_iota(jnp.int32, (size, size), 1)
    eye = jnp.eye(size, dtype=jnp.float32)
    lower = system - eye
    diagonal = jnp.where(rows // base == cols // base, lower, 0.0)
    inverse = eye - diagonal
    power = diagonal
    reach = 2
    while reach < base:
        power = matmul("...ij,...jk->...ik", power, power)
        inverse = inverse + matmul("...ij,...jk->...ik", inverse, power)
        reach *= 2
    width = base
    while width < size:
        inside = (rows // (2 * width) == cols // (2 * width)) & (rows // width != cols // width)
        coupling = jnp.where(inside, lower, 0.0)
        inverse = inverse - matmul(
            "...ij,...jk->...ik", matmul("...ij,...jk->...ik", inverse, coupling), inverse
        )
        width *= 2
    return inverse


def block_system(key_block, log_decay, beta_block):
    key_unit = key_block / jnp.sqrt(jnp.sum(key_block * key_block, axis=-1, keepdims=True) + 1e-06)
    cumulative = jnp.cumsum(log_decay, axis=-1)
    sequence_length = key_block.shape[1]
    lower_mask = jnp.tril(jnp.ones((sequence_length, sequence_length), dtype=jnp.bool_))
    strict = jnp.tril(jnp.ones((sequence_length, sequence_length), dtype=jnp.bool_), -1)
    spread = cumulative[:, :, None] - cumulative[:, None, :]
    ratios = jnp.where(lower_mask, jnp.exp(jnp.where(lower_mask, spread, 0.0)), 0.0)
    key_inner = matmul("bik,bjk->bij", key_unit, key_unit)
    system = jnp.where(strict, beta_block[:, :, None] * ratios * key_inner, 0.0) + jnp.eye(
        sequence_length, dtype=jnp.float32
    )
    return key_unit, cumulative, ratios, unit_lower_inverse(system)


def block_terms(query_block, key_block, value_block, log_decay, beta_block):
    key_unit, cumulative, ratios, system_inverse = block_system(key_block, log_decay, beta_block)
    growth = jnp.exp(cumulative)
    right_side = jnp.concatenate(
        [beta_block[:, :, None] * value_block, (beta_block * growth)[:, :, None] * key_unit],
        axis=-1,
    )
    solved = matmul("bij,bjv->biv", system_inverse, right_side)
    value_size = value_block.shape[-1]
    updates = solved[:, :, :value_size]
    weighted = solved[:, :, value_size:]
    attend = ratios * matmul("bik,bjk->bij", query_block, key_unit)
    local_out = matmul("bij,bjv->biv", attend, updates)
    state_query = growth[:, :, None] * query_block - matmul("bij,bjk->bik", attend, weighted)
    key_tail = jnp.exp(cumulative[:, -1:] - cumulative)[:, :, None] * key_unit
    return (local_out, state_query, key_tail, weighted, updates, growth[:, -1])


def column_operator(query_block, key_block, log_decay, beta_block):
    key_unit, cumulative, ratios, system_inverse = block_system(key_block, log_decay, beta_block)
    attend = ratios * matmul("bik,bjk->bij", query_block, key_unit)
    return matmul("bij,bjk->bik", attend, system_inverse) * beta_block[:, None, :]


def to_heads(array, leading_count, sequence_length, head_count, head_size):
    shaped = array.astype(jnp.float32).reshape(
        leading_count, sequence_length, head_count, head_size
    )
    return shaped.transpose(0, 2, 1, 3).reshape(
        leading_count * head_count, sequence_length, head_size
    )


def gates_to_heads(array, leading_count, sequence_length, head_count):
    return array.transpose(0, 2, 1).reshape(leading_count * head_count, sequence_length)


def from_heads(array, leading_count, sequence_length, head_count, head_size):
    return array.reshape(leading_count, head_count, sequence_length, head_size).transpose(
        0, 2, 1, 3
    )


def head_norm(array, gain):
    return array * lax.rsqrt(jnp.mean(array * array, axis=-1, keepdims=True) + 1e-05) * gain


def prefix_states(transfer, offset):
    scan_count = lax.axis_size("scan")
    head_size = offset.shape[-1]
    ahead_transfer = jnp.zeros_like(transfer)
    ahead_offset = jnp.zeros_like(offset)
    distance = 1
    while distance < scan_count:
        if 2 * distance < scan_count:
            arrived = jnp.concatenate(from_behind((transfer, offset), "scan", distance), axis=-1)
            composed = matmul("bij,bjv->biv", transfer, arrived)
            if distance == 1:
                ahead_transfer = arrived[:, :, :head_size]
                ahead_offset = arrived[:, :, head_size:]
            else:
                ahead = matmul("bij,bjv->biv", ahead_transfer, arrived)
                ahead_transfer = ahead[:, :, :head_size]
                ahead_offset = ahead[:, :, head_size:] + ahead_offset
            transfer = composed[:, :, :head_size]
            offset = composed[:, :, head_size:] + offset
        else:
            arrived = from_behind(offset, "scan", distance)
            if distance == 1:
                ahead_offset = arrived
            else:
                ahead_offset = matmul("bij,bjv->biv", ahead_transfer, arrived) + ahead_offset
        distance *= 2
    return ahead_offset


def shards(
    query_row,
    key_row,
    value_row,
    decay_row,
    beta_row,
    gain_row,
    query_col,
    key_col,
    decay_col,
    beta_col,
    gain_col,
):
    row_count, segment, features = query_row.shape
    head_size = gain_row.shape[0]
    head_count = features // head_size
    line_count = lax.axis_size("line")
    total_rows = query_col.shape[0]
    column_count = query_col.shape[2]

    def columns(array):
        return array.reshape(total_rows, column_count, -1).transpose(1, 0, 2)

    local_out, state_query, key_tail, weighted, updates, ending = block_terms(
        to_heads(query_row, row_count, segment, head_count, head_size),
        to_heads(key_row, row_count, segment, head_count, head_size),
        to_heads(value_row, row_count, segment, head_count, head_size),
        gates_to_heads(decay_row, row_count, segment, head_count),
        gates_to_heads(beta_row, row_count, segment, head_count),
    )
    identity = jnp.broadcast_to(
        jnp.eye(head_size, dtype=jnp.float32), (row_count * head_count, head_size, head_size)
    )
    transfer = ending[:, None, None] * identity - matmul("bjk,bjl->bkl", key_tail, weighted)
    offset = matmul("bjk,bjv->bkv", key_tail, updates)

    operator = column_operator(
        to_heads(columns(query_col), column_count, total_rows, head_count, head_size),
        to_heads(columns(key_col), column_count, total_rows, head_count, head_size),
        gates_to_heads(columns(decay_col), column_count, total_rows, head_count),
        gates_to_heads(columns(beta_col), column_count, total_rows, head_count),
    )

    incoming = prefix_states(transfer, offset)
    row_out = local_out + matmul("bik,bkv->biv", state_query, incoming)
    row_scan = from_heads(row_out, row_count, segment, head_count, head_size)
    values_col = (
        head_norm(row_scan, gain_row).reshape(row_count, segment, features).astype(jnp.bfloat16)
    )
    values_col, operator = lax.optimization_barrier((values_col, operator))
    arranged = values_col.reshape(row_count, line_count, segment // line_count, features)
    column_values = lax.all_to_all(arranged, "line", split_axis=1, concat_axis=0, tiled=True)

    col_out = matmul(
        "bij,bjv->biv",
        operator,
        to_heads(columns(column_values), column_count, total_rows, head_count, head_size),
    )
    col_scan = from_heads(col_out, column_count, total_rows, head_count, head_size)
    normed = (
        head_norm(col_scan, gain_col)
        .transpose(1, 0, 2, 3)
        .reshape(total_rows, 1, column_count, features)
        .astype(jnp.bfloat16)
    )
    returned = lax.all_to_all(normed, "line", split_axis=0, concat_axis=1, tiled=True)
    return returned.reshape(row_count, segment, features)


def solution(mesh):
    placed = (
        P("line", "scan", None),
        P("line", "scan", None),
        P("line", "scan", None),
        P("line", "scan", None),
        P("line", "scan", None),
        P(),
        P(None, "scan", "line", None),
        P(None, "scan", "line", None),
        P(None, "scan", "line", None),
        P(None, "scan", "line", None),
        P(),
    )
    return jax.shard_map(
        shards, mesh=mesh, in_specs=placed, out_specs=P("line", "scan", None), check_vma=False
    )
```

```python
import jax
import jax.numpy as jnp
from jax import lax
from jax.sharding import PartitionSpec as P

HIGHEST = lax.Precision.HIGHEST
BASE_BLOCK = 16


def from_behind(block, axis, distance):
    devices = range(lax.axis_size(axis))
    route = [(i - distance, i) for i in devices if i - distance in devices]
    return lax.ppermute(block, axis, route)


def matmul(spec, left, right):
    return jnp.einsum(spec, left, right, precision=HIGHEST)


def unit_lower_inverse(system):
    size = system.shape[-1]
    base = min(BASE_BLOCK, size)
    assert size % base == 0
    rows = lax.broadcasted_iota(jnp.int32, (size, size), 0)
    cols = lax.broadcasted_iota(jnp.int32, (size, size), 1)
    eye = jnp.eye(size, dtype=jnp.float32)
    lower = system - eye
    diagonal = jnp.where(rows // base == cols // base, lower, 0.0)
    inverse = eye - diagonal
    power = diagonal
    reach = 2
    while reach < base:
        power = matmul("...ij,...jk->...ik", power, power)
        inverse = inverse + matmul("...ij,...jk->...ik", inverse, power)
        reach *= 2
    width = base
    while width < size:
        inside = (rows // (2 * width) == cols // (2 * width)) & (rows // width != cols // width)
        coupling = jnp.where(inside, lower, 0.0)
        inverse = inverse - matmul(
            "...ij,...jk->...ik", matmul("...ij,...jk->...ik", inverse, coupling), inverse
        )
        width *= 2
    return inverse


def block_system(key_block, log_decay, beta_block):
    key_unit = key_block / jnp.sqrt(jnp.sum(key_block * key_block, axis=-1, keepdims=True) + 1e-06)
    cumulative = jnp.cumsum(log_decay, axis=-1)
    sequence_length = key_block.shape[1]
    lower_mask = jnp.tril(jnp.ones((sequence_length, sequence_length), dtype=jnp.bool_))
    strict = jnp.tril(jnp.ones((sequence_length, sequence_length), dtype=jnp.bool_), -1)
    spread = cumulative[:, :, None] - cumulative[:, None, :]
    ratios = jnp.where(lower_mask, jnp.exp(jnp.where(lower_mask, spread, 0.0)), 0.0)
    key_inner = matmul("bik,bjk->bij", key_unit, key_unit)
    system = jnp.where(strict, beta_block[:, :, None] * ratios * key_inner, 0.0) + jnp.eye(
        sequence_length, dtype=jnp.float32
    )
    return key_unit, cumulative, ratios, unit_lower_inverse(system)


def block_terms(query_block, key_block, value_block, log_decay, beta_block):
    key_unit, cumulative, ratios, system_inverse = block_system(key_block, log_decay, beta_block)
    growth = jnp.exp(cumulative)
    right_side = jnp.concatenate(
        [beta_block[:, :, None] * value_block, (beta_block * growth)[:, :, None] * key_unit],
        axis=-1,
    )
    solved = matmul("bij,bjv->biv", system_inverse, right_side)
    value_size = value_block.shape[-1]
    updates = solved[:, :, :value_size]
    weighted = solved[:, :, value_size:]
    attend = ratios * matmul("bik,bjk->bij", query_block, key_unit)
    local_out = matmul("bij,bjv->biv", attend, updates)
    state_query = growth[:, :, None] * query_block - matmul("bij,bjk->bik", attend, weighted)
    key_tail = jnp.exp(cumulative[:, -1:] - cumulative)[:, :, None] * key_unit
    return (local_out, state_query, key_tail, weighted, updates, growth[:, -1])


def column_operator(query_block, key_block, log_decay, beta_block):
    key_unit, cumulative, ratios, system_inverse = block_system(key_block, log_decay, beta_block)
    attend = ratios * matmul("bik,bjk->bij", query_block, key_unit)
    return matmul("bij,bjk->bik", attend, system_inverse) * beta_block[:, None, :]


def to_heads(array, leading_count, sequence_length, head_count, head_size):
    shaped = array.astype(jnp.float32).reshape(
        leading_count, sequence_length, head_count, head_size
    )
    return shaped.transpose(0, 2, 1, 3).reshape(
        leading_count * head_count, sequence_length, head_size
    )


def gates_to_heads(array, leading_count, sequence_length, head_count):
    return array.transpose(0, 2, 1).reshape(leading_count * head_count, sequence_length)


def from_heads(array, leading_count, sequence_length, head_count, head_size):
    return array.reshape(leading_count, head_count, sequence_length, head_size).transpose(
        0, 2, 1, 3
    )


def head_norm(array, gain):
    return array * lax.rsqrt(jnp.mean(array * array, axis=-1, keepdims=True) + 1e-05) * gain


def split_heads(array):
    half = array.shape[0] // 2 if array.shape[0] % 2 == 0 else array.shape[0]
    return tuple(array[start:start + half] for start in range(0, array.shape[0], half))


def prefix_states(transfer, offset):
    scan_count = lax.axis_size("scan")
    head_size = offset.shape[-1]
    ahead_transfer = jnp.zeros_like(transfer)
    ahead_offset = jnp.zeros_like(offset)
    distance = 1
    while distance < scan_count:
        if 2 * distance < scan_count:
            arrived = jnp.concatenate(
                [
                    jnp.concatenate(from_behind(split_heads(part), "scan", distance), axis=0)
                    for part in (transfer, offset)
                ],
                axis=-1,
            )
            composed = matmul("bij,bjv->biv", transfer, arrived)
            if distance == 1:
                ahead_transfer = arrived[:, :, :head_size]
                ahead_offset = arrived[:, :, head_size:]
            else:
                ahead = matmul("bij,bjv->biv", ahead_transfer, arrived)
                ahead_transfer = ahead[:, :, :head_size]
                ahead_offset = ahead[:, :, head_size:] + ahead_offset
            transfer = composed[:, :, :head_size]
            offset = composed[:, :, head_size:] + offset
        else:
            arrived = jnp.concatenate(from_behind(split_heads(offset), "scan", distance), axis=0)
            if distance == 1:
                ahead_offset = arrived
            else:
                ahead_offset = matmul("bij,bjv->biv", ahead_transfer, arrived) + ahead_offset
        distance *= 2
    return ahead_offset


def shards(
    query_row,
    key_row,
    value_row,
    decay_row,
    beta_row,
    gain_row,
    query_col,
    key_col,
    decay_col,
    beta_col,
    gain_col,
):
    row_count, segment, features = query_row.shape
    head_size = gain_row.shape[0]
    head_count = features // head_size
    line_count = lax.axis_size("line")
    total_rows = query_col.shape[0]
    column_count = query_col.shape[2]

    def columns(array):
        return array.reshape(total_rows, column_count, -1).transpose(1, 0, 2)

    local_out, state_query, key_tail, weighted, updates, ending = block_terms(
        to_heads(query_row, row_count, segment, head_count, head_size),
        to_heads(key_row, row_count, segment, head_count, head_size),
        to_heads(value_row, row_count, segment, head_count, head_size),
        gates_to_heads(decay_row, row_count, segment, head_count),
        gates_to_heads(beta_row, row_count, segment, head_count),
    )
    identity = jnp.broadcast_to(
        jnp.eye(head_size, dtype=jnp.float32), (row_count * head_count, head_size, head_size)
    )
    transfer = ending[:, None, None] * identity - matmul("bjk,bjl->bkl", key_tail, weighted)
    offset = matmul("bjk,bjv->bkv", key_tail, updates)

    operator = column_operator(
        to_heads(columns(query_col), column_count, total_rows, head_count, head_size),
        to_heads(columns(key_col), column_count, total_rows, head_count, head_size),
        gates_to_heads(columns(decay_col), column_count, total_rows, head_count),
        gates_to_heads(columns(beta_col), column_count, total_rows, head_count),
    )

    incoming = prefix_states(transfer, offset)
    row_out = local_out + matmul("bik,bkv->biv", state_query, incoming)
    row_scan = from_heads(row_out, row_count, segment, head_count, head_size)
    values_col = (
        head_norm(row_scan, gain_row).reshape(row_count, segment, features).astype(jnp.bfloat16)
    )
    values_col, operator = lax.optimization_barrier((values_col, operator))
    arranged = values_col.reshape(row_count, line_count, segment // line_count, features)
    column_values = lax.all_to_all(arranged, "line", split_axis=1, concat_axis=0, tiled=True)

    col_out = matmul(
        "bij,bjv->biv",
        operator,
        to_heads(columns(column_values), column_count, total_rows, head_count, head_size),
    )
    col_scan = from_heads(col_out, column_count, total_rows, head_count, head_size)
    normed = (
        head_norm(col_scan, gain_col)
        .transpose(1, 0, 2, 3)
        .reshape(total_rows, 1, column_count, features)
        .astype(jnp.bfloat16)
    )
    returned = lax.all_to_all(normed, "line", split_axis=0, concat_axis=1, tiled=True)
    return returned.reshape(row_count, segment, features)


def solution(mesh):
    placed = (
        P("line", "scan", None),
        P("line", "scan", None),
        P("line", "scan", None),
        P("line", "scan", None),
        P("line", "scan", None),
        P(),
        P(None, "scan", "line", None),
        P(None, "scan", "line", None),
        P(None, "scan", "line", None),
        P(None, "scan", "line", None),
        P(),
    )
    return jax.shard_map(
        shards, mesh=mesh, in_specs=placed, out_specs=P("line", "scan", None), check_vma=False
    )
```

```python
import jax
import jax.numpy as jnp
from jax import lax
from jax.sharding import PartitionSpec as P

HIGHEST = lax.Precision.HIGHEST
BASE_BLOCK = 16


def from_behind(block, axis, distance):
    devices = range(lax.axis_size(axis))
    route = [(i - distance, i) for i in devices if i - distance in devices]
    return lax.ppermute(block, axis, route)


def matmul(spec, left, right):
    return jnp.einsum(spec, left, right, precision=HIGHEST)


def unit_lower_inverse(system):
    size = system.shape[-1]
    base = min(BASE_BLOCK, size)
    assert size % base == 0
    rows = lax.broadcasted_iota(jnp.int32, (size, size), 0)
    cols = lax.broadcasted_iota(jnp.int32, (size, size), 1)
    eye = jnp.eye(size, dtype=jnp.float32)
    lower = system - eye
    diagonal = jnp.where(rows // base == cols // base, lower, 0.0)
    inverse = eye - diagonal
    power = diagonal
    reach = 2
    while reach < base:
        power = matmul("...ij,...jk->...ik", power, power)
        inverse = inverse + matmul("...ij,...jk->...ik", inverse, power)
        reach *= 2
    width = base
    while width < size:
        inside = (rows // (2 * width) == cols // (2 * width)) & (rows // width != cols // width)
        coupling = jnp.where(inside, lower, 0.0)
        inverse = inverse - matmul(
            "...ij,...jk->...ik", matmul("...ij,...jk->...ik", inverse, coupling), inverse
        )
        width *= 2
    return inverse


def block_system(key_block, log_decay, beta_block):
    key_unit = key_block / jnp.sqrt(jnp.sum(key_block * key_block, axis=-1, keepdims=True) + 1e-06)
    cumulative = jnp.cumsum(log_decay, axis=-1)
    sequence_length = key_block.shape[1]
    lower_mask = jnp.tril(jnp.ones((sequence_length, sequence_length), dtype=jnp.bool_))
    strict = jnp.tril(jnp.ones((sequence_length, sequence_length), dtype=jnp.bool_), -1)
    spread = cumulative[:, :, None] - cumulative[:, None, :]
    ratios = jnp.where(lower_mask, jnp.exp(jnp.where(lower_mask, spread, 0.0)), 0.0)
    key_inner = matmul("bik,bjk->bij", key_unit, key_unit)
    system = jnp.where(strict, beta_block[:, :, None] * ratios * key_inner, 0.0) + jnp.eye(
        sequence_length, dtype=jnp.float32
    )
    return key_unit, cumulative, ratios, unit_lower_inverse(system)


def block_terms(query_block, key_block, value_block, log_decay, beta_block):
    key_unit, cumulative, ratios, system_inverse = block_system(key_block, log_decay, beta_block)
    growth = jnp.exp(cumulative)
    right_side = jnp.concatenate(
        [beta_block[:, :, None] * value_block, (beta_block * growth)[:, :, None] * key_unit],
        axis=-1,
    )
    solved = matmul("bij,bjv->biv", system_inverse, right_side)
    value_size = value_block.shape[-1]
    updates = solved[:, :, :value_size]
    weighted = solved[:, :, value_size:]
    attend = ratios * matmul("bik,bjk->bij", query_block, key_unit)
    local_out = matmul("bij,bjv->biv", attend, updates)
    state_query = growth[:, :, None] * query_block - matmul("bij,bjk->bik", attend, weighted)
    key_tail = jnp.exp(cumulative[:, -1:] - cumulative)[:, :, None] * key_unit
    return (local_out, state_query, key_tail, weighted, updates, growth[:, -1])


def column_operator(query_block, key_block, log_decay, beta_block):
    key_unit, cumulative, ratios, system_inverse = block_system(key_block, log_decay, beta_block)
    attend = ratios * matmul("bik,bjk->bij", query_block, key_unit)
    return matmul("bij,bjk->bik", attend, system_inverse) * beta_block[:, None, :]


def to_heads(array, leading_count, sequence_length, head_count, head_size):
    shaped = array.astype(jnp.float32).reshape(
        leading_count, sequence_length, head_count, head_size
    )
    return shaped.transpose(0, 2, 1, 3).reshape(
        leading_count * head_count, sequence_length, head_size
    )


def gates_to_heads(array, leading_count, sequence_length, head_count):
    return array.transpose(0, 2, 1).reshape(leading_count * head_count, sequence_length)


def from_heads(array, leading_count, sequence_length, head_count, head_size):
    return array.reshape(leading_count, head_count, sequence_length, head_size).transpose(
        0, 2, 1, 3
    )


def head_norm(array, gain):
    return array * lax.rsqrt(jnp.mean(array * array, axis=-1, keepdims=True) + 1e-05) * gain


def split_heads(array):
    half = array.shape[0] // 2 if array.shape[0] % 2 == 0 else array.shape[0]
    return tuple(array[start:start + half] for start in range(0, array.shape[0], half))


def prefix_states(transfer, offset):
    scan_count = lax.axis_size("scan")
    head_size = offset.shape[-1]
    ahead_transfer = jnp.zeros_like(transfer)
    ahead_offset = jnp.zeros_like(offset)
    distance = 1
    while distance < scan_count:
        if 2 * distance < scan_count:
            arrived = jnp.concatenate(from_behind((transfer, offset), "scan", distance), axis=-1)
            composed = matmul("bij,bjv->biv", transfer, arrived)
            if distance == 1:
                ahead_transfer = arrived[:, :, :head_size]
                ahead_offset = arrived[:, :, head_size:]
            else:
                ahead = matmul("bij,bjv->biv", ahead_transfer, arrived)
                ahead_transfer = ahead[:, :, :head_size]
                ahead_offset = ahead[:, :, head_size:] + ahead_offset
            transfer = composed[:, :, :head_size]
            offset = composed[:, :, head_size:] + offset
        else:
            arrived = jnp.concatenate(from_behind(split_heads(offset), "scan", distance), axis=0)
            if distance == 1:
                ahead_offset = arrived
            else:
                ahead_offset = matmul("bij,bjv->biv", ahead_transfer, arrived) + ahead_offset
        distance *= 2
    return ahead_offset


def shards(
    query_row,
    key_row,
    value_row,
    decay_row,
    beta_row,
    gain_row,
    query_col,
    key_col,
    decay_col,
    beta_col,
    gain_col,
):
    row_count, segment, features = query_row.shape
    head_size = gain_row.shape[0]
    head_count = features // head_size
    line_count = lax.axis_size("line")
    total_rows = query_col.shape[0]
    column_count = query_col.shape[2]

    def columns(array):
        return array.reshape(total_rows, column_count, -1).transpose(1, 0, 2)

    local_out, state_query, key_tail, weighted, updates, ending = block_terms(
        to_heads(query_row, row_count, segment, head_count, head_size),
        to_heads(key_row, row_count, segment, head_count, head_size),
        to_heads(value_row, row_count, segment, head_count, head_size),
        gates_to_heads(decay_row, row_count, segment, head_count),
        gates_to_heads(beta_row, row_count, segment, head_count),
    )
    identity = jnp.broadcast_to(
        jnp.eye(head_size, dtype=jnp.float32), (row_count * head_count, head_size, head_size)
    )
    transfer = ending[:, None, None] * identity - matmul("bjk,bjl->bkl", key_tail, weighted)
    offset = matmul("bjk,bjv->bkv", key_tail, updates)

    operator = column_operator(
        to_heads(columns(query_col), column_count, total_rows, head_count, head_size),
        to_heads(columns(key_col), column_count, total_rows, head_count, head_size),
        gates_to_heads(columns(decay_col), column_count, total_rows, head_count),
        gates_to_heads(columns(beta_col), column_count, total_rows, head_count),
    )

    incoming = prefix_states(transfer, offset)
    row_out = local_out + matmul("bik,bkv->biv", state_query, incoming)
    row_scan = from_heads(row_out, row_count, segment, head_count, head_size)
    values_col = (
        head_norm(row_scan, gain_row).reshape(row_count, segment, features).astype(jnp.bfloat16)
    )
    values_col, operator = lax.optimization_barrier((values_col, operator))
    arranged = values_col.reshape(row_count, line_count, segment // line_count, features)
    column_values = lax.all_to_all(arranged, "line", split_axis=1, concat_axis=0, tiled=True)

    col_out = matmul(
        "bij,bjv->biv",
        operator,
        to_heads(columns(column_values), column_count, total_rows, head_count, head_size),
    )
    col_scan = from_heads(col_out, column_count, total_rows, head_count, head_size)
    normed = (
        head_norm(col_scan, gain_col)
        .transpose(1, 0, 2, 3)
        .reshape(total_rows, 1, column_count, features)
        .astype(jnp.bfloat16)
    )
    returned = lax.all_to_all(normed, "line", split_axis=0, concat_axis=1, tiled=True)
    return returned.reshape(row_count, segment, features)


def solution(mesh):
    placed = (
        P("line", "scan", None),
        P("line", "scan", None),
        P("line", "scan", None),
        P("line", "scan", None),
        P("line", "scan", None),
        P(),
        P(None, "scan", "line", None),
        P(None, "scan", "line", None),
        P(None, "scan", "line", None),
        P(None, "scan", "line", None),
        P(),
    )
    return jax.shard_map(
        shards, mesh=mesh, in_specs=placed, out_specs=P("line", "scan", None), check_vma=False
    )
```

```python
import jax
import jax.numpy as jnp
from jax import lax
from jax.sharding import PartitionSpec as P

HIGHEST = lax.Precision.HIGHEST
BASE_BLOCK = 16


def from_behind(block, axis, distance):
    devices = range(lax.axis_size(axis))
    route = [(i - distance, i) for i in devices if i - distance in devices]
    return lax.ppermute(block, axis, route)


def matmul(spec, left, right):
    return jnp.einsum(spec, left, right, precision=HIGHEST)


def unit_lower_inverse(system):
    size = system.shape[-1]
    base = min(BASE_BLOCK, size)
    assert size % base == 0
    rows = lax.broadcasted_iota(jnp.int32, (size, size), 0)
    cols = lax.broadcasted_iota(jnp.int32, (size, size), 1)
    eye = jnp.eye(size, dtype=jnp.float32)
    lower = system - eye
    diagonal = jnp.where(rows // base == cols // base, lower, 0.0)
    inverse = eye - diagonal
    power = diagonal
    reach = 2
    while reach < base:
        power = matmul("...ij,...jk->...ik", power, power)
        inverse = inverse + matmul("...ij,...jk->...ik", inverse, power)
        reach *= 2
    width = base
    while width < size:
        inside = (rows // (2 * width) == cols // (2 * width)) & (rows // width != cols // width)
        coupling = jnp.where(inside, lower, 0.0)
        inverse = inverse - matmul(
            "...ij,...jk->...ik", matmul("...ij,...jk->...ik", inverse, coupling), inverse
        )
        width *= 2
    return inverse


def block_system(key_block, log_decay, beta_block):
    key_unit = key_block / jnp.sqrt(jnp.sum(key_block * key_block, axis=-1, keepdims=True) + 1e-06)
    cumulative = jnp.cumsum(log_decay, axis=-1)
    sequence_length = key_block.shape[1]
    lower_mask = jnp.tril(jnp.ones((sequence_length, sequence_length), dtype=jnp.bool_))
    strict = jnp.tril(jnp.ones((sequence_length, sequence_length), dtype=jnp.bool_), -1)
    spread = cumulative[:, :, None] - cumulative[:, None, :]
    ratios = jnp.where(lower_mask, jnp.exp(jnp.where(lower_mask, spread, 0.0)), 0.0)
    key_inner = matmul("bik,bjk->bij", key_unit, key_unit)
    system = jnp.where(strict, beta_block[:, :, None] * ratios * key_inner, 0.0) + jnp.eye(
        sequence_length, dtype=jnp.float32
    )
    return key_unit, cumulative, ratios, unit_lower_inverse(system)


def block_terms(query_block, key_block, value_block, log_decay, beta_block):
    key_unit, cumulative, ratios, system_inverse = block_system(key_block, log_decay, beta_block)
    growth = jnp.exp(cumulative)
    right_side = jnp.concatenate(
        [beta_block[:, :, None] * value_block, (beta_block * growth)[:, :, None] * key_unit],
        axis=-1,
    )
    solved = matmul("bij,bjv->biv", system_inverse, right_side)
    value_size = value_block.shape[-1]
    updates = solved[:, :, :value_size]
    weighted = solved[:, :, value_size:]
    attend = ratios * matmul("bik,bjk->bij", query_block, key_unit)
    attended = matmul("bij,bjv->biv", attend, solved)
    local_out = attended[:, :, :value_size]
    state_query = growth[:, :, None] * query_block - attended[:, :, value_size:]
    key_tail = jnp.exp(cumulative[:, -1:] - cumulative)[:, :, None] * key_unit
    return (local_out, state_query, key_tail, solved, growth[:, -1])


def column_operator(query_block, key_block, log_decay, beta_block):
    key_unit, cumulative, ratios, system_inverse = block_system(key_block, log_decay, beta_block)
    attend = ratios * matmul("bik,bjk->bij", query_block, key_unit)
    return matmul("bij,bjk->bik", attend, system_inverse) * beta_block[:, None, :]


def to_heads(array, leading_count, sequence_length, head_count, head_size):
    shaped = array.astype(jnp.float32).reshape(
        leading_count, sequence_length, head_count, head_size
    )
    return shaped.transpose(0, 2, 1, 3).reshape(
        leading_count * head_count, sequence_length, head_size
    )


def gates_to_heads(array, leading_count, sequence_length, head_count):
    return array.transpose(0, 2, 1).reshape(leading_count * head_count, sequence_length)


def from_heads(array, leading_count, sequence_length, head_count, head_size):
    return array.reshape(leading_count, head_count, sequence_length, head_size).transpose(
        0, 2, 1, 3
    )


def head_norm(array, gain):
    return array * lax.rsqrt(jnp.mean(array * array, axis=-1, keepdims=True) + 1e-05) * gain


def prefix_states(transfer, offset):
    scan_count = lax.axis_size("scan")
    head_size = offset.shape[-1]
    ahead_transfer = jnp.zeros_like(transfer)
    ahead_offset = jnp.zeros_like(offset)
    distance = 1
    while distance < scan_count:
        if 2 * distance < scan_count:
            arrived = jnp.concatenate(from_behind((transfer, offset), "scan", distance), axis=-1)
            composed = matmul("bij,bjv->biv", transfer, arrived)
            if distance == 1:
                ahead_transfer = arrived[:, :, :head_size]
                ahead_offset = arrived[:, :, head_size:]
            else:
                ahead = matmul("bij,bjv->biv", ahead_transfer, arrived)
                ahead_transfer = ahead[:, :, :head_size]
                ahead_offset = ahead[:, :, head_size:] + ahead_offset
            transfer = composed[:, :, :head_size]
            offset = composed[:, :, head_size:] + offset
        else:
            arrived = from_behind(offset, "scan", distance)
            if distance == 1:
                ahead_offset = arrived
            else:
                ahead_offset = matmul("bij,bjv->biv", ahead_transfer, arrived) + ahead_offset
        distance *= 2
    return ahead_offset


def shards(
    query_row,
    key_row,
    value_row,
    decay_row,
    beta_row,
    gain_row,
    query_col,
    key_col,
    decay_col,
    beta_col,
    gain_col,
):
    row_count, segment, features = query_row.shape
    head_size = gain_row.shape[0]
    head_count = features // head_size
    line_count = lax.axis_size("line")
    total_rows = query_col.shape[0]
    column_count = query_col.shape[2]

    def columns(array):
        return array.reshape(total_rows, column_count, -1).transpose(1, 0, 2)

    local_out, state_query, key_tail, solved, ending = block_terms(
        to_heads(query_row, row_count, segment, head_count, head_size),
        to_heads(key_row, row_count, segment, head_count, head_size),
        to_heads(value_row, row_count, segment, head_count, head_size),
        gates_to_heads(decay_row, row_count, segment, head_count),
        gates_to_heads(beta_row, row_count, segment, head_count),
    )
    identity = jnp.broadcast_to(
        jnp.eye(head_size, dtype=jnp.float32), (row_count * head_count, head_size, head_size)
    )
    tail_solved = matmul("bjk,bjv->bkv", key_tail, solved)
    transfer = ending[:, None, None] * identity - tail_solved[:, :, head_size:]
    offset = tail_solved[:, :, :head_size]

    operator = column_operator(
        to_heads(columns(query_col), column_count, total_rows, head_count, head_size),
        to_heads(columns(key_col), column_count, total_rows, head_count, head_size),
        gates_to_heads(columns(decay_col), column_count, total_rows, head_count),
        gates_to_heads(columns(beta_col), column_count, total_rows, head_count),
    )

    incoming = prefix_states(transfer, offset)
    row_out = local_out + matmul("bik,bkv->biv", state_query, incoming)
    row_scan = from_heads(row_out, row_count, segment, head_count, head_size)
    values_col = (
        head_norm(row_scan, gain_row).reshape(row_count, segment, features).astype(jnp.bfloat16)
    )
    values_col, operator = lax.optimization_barrier((values_col, operator))
    arranged = values_col.reshape(row_count, line_count, segment // line_count, features)
    column_values = lax.all_to_all(arranged, "line", split_axis=1, concat_axis=0, tiled=True)

    col_out = matmul(
        "bij,bjv->biv",
        operator,
        to_heads(columns(column_values), column_count, total_rows, head_count, head_size),
    )
    col_scan = from_heads(col_out, column_count, total_rows, head_count, head_size)
    normed = (
        head_norm(col_scan, gain_col)
        .transpose(1, 0, 2, 3)
        .reshape(total_rows, 1, column_count, features)
        .astype(jnp.bfloat16)
    )
    returned = lax.all_to_all(normed, "line", split_axis=0, concat_axis=1, tiled=True)
    return returned.reshape(row_count, segment, features)


def solution(mesh):
    placed = (
        P("line", "scan", None),
        P("line", "scan", None),
        P("line", "scan", None),
        P("line", "scan", None),
        P("line", "scan", None),
        P(),
        P(None, "scan", "line", None),
        P(None, "scan", "line", None),
        P(None, "scan", "line", None),
        P(None, "scan", "line", None),
        P(),
    )
    return jax.shard_map(
        shards, mesh=mesh, in_specs=placed, out_specs=P("line", "scan", None), check_vma=False
    )
```

```python
import jax
import jax.numpy as jnp
from jax import lax
from jax.sharding import PartitionSpec as P

HIGHEST = lax.Precision.HIGHEST
BASE_BLOCK = 16


def from_behind(block, axis, distance):
    devices = range(lax.axis_size(axis))
    route = [(i - distance, i) for i in devices if i - distance in devices]
    return lax.ppermute(block, axis, route)


def matmul(spec, left, right):
    return jnp.einsum(spec, left, right, precision=HIGHEST)


def unit_lower_inverse(system):
    size = system.shape[-1]
    base = min(BASE_BLOCK, size)
    assert size % base == 0
    rows = lax.broadcasted_iota(jnp.int32, (size, size), 0)
    cols = lax.broadcasted_iota(jnp.int32, (size, size), 1)
    eye = jnp.eye(size, dtype=jnp.float32)
    lower = system - eye
    diagonal = jnp.where(rows // base == cols // base, lower, 0.0)
    inverse = eye - diagonal
    power = diagonal
    reach = 2
    while reach < base:
        power = matmul("...ij,...jk->...ik", power, power)
        inverse = inverse + matmul("...ij,...jk->...ik", inverse, power)
        reach *= 2
    width = base
    while width < size:
        inside = (rows // (2 * width) == cols // (2 * width)) & (rows // width != cols // width)
        coupling = jnp.where(inside, lower, 0.0)
        inverse = inverse - matmul(
            "...ij,...jk->...ik", matmul("...ij,...jk->...ik", inverse, coupling), inverse
        )
        width *= 2
    return inverse


def block_system(key_block, log_decay, beta_block):
    key_unit = key_block / jnp.sqrt(jnp.sum(key_block * key_block, axis=-1, keepdims=True) + 1e-06)
    cumulative = jnp.cumsum(log_decay, axis=-1)
    sequence_length = key_block.shape[1]
    lower_mask = jnp.tril(jnp.ones((sequence_length, sequence_length), dtype=jnp.bool_))
    strict = jnp.tril(jnp.ones((sequence_length, sequence_length), dtype=jnp.bool_), -1)
    spread = cumulative[:, :, None] - cumulative[:, None, :]
    ratios = jnp.where(lower_mask, jnp.exp(jnp.where(lower_mask, spread, 0.0)), 0.0)
    key_inner = matmul("bik,bjk->bij", key_unit, key_unit)
    system = jnp.where(strict, beta_block[:, :, None] * ratios * key_inner, 0.0) + jnp.eye(
        sequence_length, dtype=jnp.float32
    )
    return key_unit, cumulative, ratios, unit_lower_inverse(system)


def block_terms(query_block, key_block, value_block, log_decay, beta_block):
    key_unit, cumulative, ratios, system_inverse = block_system(key_block, log_decay, beta_block)
    growth = jnp.exp(cumulative)
    right_side = jnp.concatenate(
        [beta_block[:, :, None] * value_block, (beta_block * growth)[:, :, None] * key_unit],
        axis=-1,
    )
    solved = matmul("bij,bjv->biv", system_inverse, right_side)
    value_size = value_block.shape[-1]
    updates = solved[:, :, :value_size]
    weighted = solved[:, :, value_size:]
    attend = ratios * matmul("bik,bjk->bij", query_block, key_unit)
    attended = matmul("bij,bjv->biv", attend, solved)
    local_out = attended[:, :, :value_size]
    state_query = growth[:, :, None] * query_block - attended[:, :, value_size:]
    key_tail = jnp.exp(cumulative[:, -1:] - cumulative)[:, :, None] * key_unit
    return (local_out, state_query, key_tail, solved, growth[:, -1])


def column_operator(query_block, key_block, log_decay, beta_block):
    key_unit, cumulative, ratios, system_inverse = block_system(key_block, log_decay, beta_block)
    attend = ratios * matmul("bik,bjk->bij", query_block, key_unit)
    return matmul("bij,bjk->bik", attend, system_inverse) * beta_block[:, None, :]


def to_heads(array, leading_count, sequence_length, head_count, head_size):
    shaped = array.astype(jnp.float32).reshape(
        leading_count, sequence_length, head_count, head_size
    )
    return shaped.transpose(0, 2, 1, 3).reshape(
        leading_count * head_count, sequence_length, head_size
    )


def gates_to_heads(array, leading_count, sequence_length, head_count):
    return array.transpose(0, 2, 1).reshape(leading_count * head_count, sequence_length)


def from_heads(array, leading_count, sequence_length, head_count, head_size):
    return array.reshape(leading_count, head_count, sequence_length, head_size).transpose(
        0, 2, 1, 3
    )


def head_norm(array, gain):
    return array * lax.rsqrt(jnp.mean(array * array, axis=-1, keepdims=True) + 1e-05) * gain


def prefix_states(transfer, offset):
    scan_count = lax.axis_size("scan")
    head_size = offset.shape[-1]
    ahead_transfer = jnp.zeros_like(transfer)
    ahead_offset = jnp.zeros_like(offset)
    distance = 1
    while distance < scan_count:
        if 2 * distance < scan_count:
            if distance == 1:
                arrived = from_behind(jnp.concatenate([transfer, offset], axis=-1), "scan", distance)
            else:
                arrived = jnp.concatenate(
                    from_behind((transfer, offset), "scan", distance), axis=-1
                )
            composed = matmul("bij,bjv->biv", transfer, arrived)
            if distance == 1:
                ahead_transfer = arrived[:, :, :head_size]
                ahead_offset = arrived[:, :, head_size:]
            else:
                ahead = matmul("bij,bjv->biv", ahead_transfer, arrived)
                ahead_transfer = ahead[:, :, :head_size]
                ahead_offset = ahead[:, :, head_size:] + ahead_offset
            transfer = composed[:, :, :head_size]
            offset = composed[:, :, head_size:] + offset
        else:
            arrived = from_behind(offset, "scan", distance)
            if distance == 1:
                ahead_offset = arrived
            else:
                ahead_offset = matmul("bij,bjv->biv", ahead_transfer, arrived) + ahead_offset
        distance *= 2
    return ahead_offset


def shards(
    query_row,
    key_row,
    value_row,
    decay_row,
    beta_row,
    gain_row,
    query_col,
    key_col,
    decay_col,
    beta_col,
    gain_col,
):
    row_count, segment, features = query_row.shape
    head_size = gain_row.shape[0]
    head_count = features // head_size
    line_count = lax.axis_size("line")
    total_rows = query_col.shape[0]
    column_count = query_col.shape[2]

    def columns(array):
        return array.reshape(total_rows, column_count, -1).transpose(1, 0, 2)

    local_out, state_query, key_tail, solved, ending = block_terms(
        to_heads(query_row, row_count, segment, head_count, head_size),
        to_heads(key_row, row_count, segment, head_count, head_size),
        to_heads(value_row, row_count, segment, head_count, head_size),
        gates_to_heads(decay_row, row_count, segment, head_count),
        gates_to_heads(beta_row, row_count, segment, head_count),
    )
    identity = jnp.broadcast_to(
        jnp.eye(head_size, dtype=jnp.float32), (row_count * head_count, head_size, head_size)
    )
    tail_solved = matmul("bjk,bjv->bkv", key_tail, solved)
    transfer = ending[:, None, None] * identity - tail_solved[:, :, head_size:]
    offset = tail_solved[:, :, :head_size]

    operator = column_operator(
        to_heads(columns(query_col), column_count, total_rows, head_count, head_size),
        to_heads(columns(key_col), column_count, total_rows, head_count, head_size),
        gates_to_heads(columns(decay_col), column_count, total_rows, head_count),
        gates_to_heads(columns(beta_col), column_count, total_rows, head_count),
    )

    incoming = prefix_states(transfer, offset)
    row_out = local_out + matmul("bik,bkv->biv", state_query, incoming)
    row_scan = from_heads(row_out, row_count, segment, head_count, head_size)
    values_col = (
        head_norm(row_scan, gain_row).reshape(row_count, segment, features).astype(jnp.bfloat16)
    )
    values_col, operator = lax.optimization_barrier((values_col, operator))
    arranged = values_col.reshape(row_count, line_count, segment // line_count, features)
    column_values = lax.all_to_all(arranged, "line", split_axis=1, concat_axis=0, tiled=True)

    col_out = matmul(
        "bij,bjv->biv",
        operator,
        to_heads(columns(column_values), column_count, total_rows, head_count, head_size),
    )
    col_scan = from_heads(col_out, column_count, total_rows, head_count, head_size)
    normed = (
        head_norm(col_scan, gain_col)
        .transpose(1, 0, 2, 3)
        .reshape(total_rows, 1, column_count, features)
        .astype(jnp.bfloat16)
    )
    returned = lax.all_to_all(normed, "line", split_axis=0, concat_axis=1, tiled=True)
    return returned.reshape(row_count, segment, features)


def solution(mesh):
    placed = (
        P("line", "scan", None),
        P("line", "scan", None),
        P("line", "scan", None),
        P("line", "scan", None),
        P("line", "scan", None),
        P(),
        P(None, "scan", "line", None),
        P(None, "scan", "line", None),
        P(None, "scan", "line", None),
        P(None, "scan", "line", None),
        P(),
    )
    return jax.shard_map(
        shards, mesh=mesh, in_specs=placed, out_specs=P("line", "scan", None), check_vma=False
    )
```
